512 devices in a mesh: pipe: 16 (over z), seq: 8 (over y, core), dp: 4 (over x).
Axes of the slice: x: 4, y: 4, z: 16, core: 2. Of those that a mesh axis runs over, the one named last changes fastest.
Arguments:
- acts: bfloat16 [16, 4, 1024, 8192], P('pipe', 'dp', 'seq'), may hold values from -6 to 6
- top_grad: bfloat16 [4, 1024, 8192], P('dp', 'seq'), may hold values from -6 to 6
- a_rows: bfloat16 [16, 32, 8192], P('pipe', None, ('seq', 'dp')), may hold values from -1 to 1
- b_rows: bfloat16 [16, 32, 8192], P('pipe', None, ('seq', 'dp')), may hold values from -0.375 to 0.375
- gain: bfloat16 [16, 8192], P('pipe', ('seq', 'dp')), may hold values from 0.5 to 1.5
Outputs:
- grad_a: float32 [16, 32, 8192], P('pipe', None, ('seq', 'dp'))
- grad_b: float32 [16, 32, 8192], P('pipe', None, ('seq', 'dp'))
- grad_gain: float32 [16, 8192], P('pipe', ('seq', 'dp'))
- clip_factors: float32 [4], P('dp')
The draws below stay inside these ranges and needn't reach their ends.
All inputs are finite; a program needn't handle non-finite values.
Results may differ from the reference program's by a relative error of at most 0.019.
Values may be sent and summed in bfloat16 or wider, within the bound.
No kernel may reach another device: no remote copies, remote signals or barrier semaphores. Data moves between devices by JAX's collectives and lax.ppermute only.
A program may use at most 64 MiB of HBM per device.

```python
import math
import jax
import jax.numpy as jnp
from jax import lax

D = 8192
RANK = 32
LEN = 1024
SECTIONS = 16
EXAMPLES = 4
N_PIPE = 16
N_DP = 4


def shared_direction(key):
    direction = jax.random.normal(jax.random.fold_in(key, 11), (SECTIONS, D), jnp.float32)
    return jnp.clip(direction, -4.0, 4.0)


def draw_a_rows(key, part):
    direction = shared_direction(key)
    private_part = jnp.clip(jax.random.normal(jax.random.fold_in(key, 12), (SECTIONS, RANK, D), jnp.float32), -4.0, 4.0)
    combined = (private_part + 0.5 * direction[:, None, :]) * (1.0 / math.sqrt(D))
    return combined.astype(jnp.bfloat16)


def draw_acts(key, part):
    direction = shared_direction(key)
    example_sign = jax.random.rademacher(jax.random.fold_in(key, 13), (EXAMPLES,), jnp.float32)
    base_noise = jnp.clip(jax.random.normal(jax.random.fold_in(key, 14), (SECTIONS, EXAMPLES, LEN, D), jnp.float32), -4.5, 4.5)
    combined = base_noise + example_sign[None, :, None, None] * direction[:, None, None, :]
    return jnp.clip(combined, -6.0, 6.0).astype(jnp.bfloat16)


def levels(key, shape, split, least, largest):
    factor_of, own = 1.0, jax.random.fold_in(key, 6)
    for dim, shards_of in split:
        heights = jnp.exp(jax.random.uniform(jax.random.fold_in(own, dim), (shards_of,), jnp.float32, least / len(split), largest / len(split)))
        factor_of = factor_of * jnp.repeat(heights, shape[dim] // shards_of).reshape([-1 if axis == dim else 1 for axis in range(len(shape))])
    return factor_of


def centred(rng, extent, width, limit, cuts=(), dtype=jnp.bfloat16):
    factor_of = levels(rng, extent, cuts, -0.22, 0.18) if cuts else 1.0
    values = jax.random.normal(rng, extent, jnp.float32) * width * factor_of
    return jnp.minimum(jnp.maximum(values, -limit), limit).astype(dtype)


def setup_inputs(seed: int = 0) -> dict:
    streams_of = jax.random.split(jax.random.key(seed), 6)
    acts = draw_acts(jax.random.fold_in(streams_of[5], 71), 0)
    top_grad = centred(streams_of[1], (EXAMPLES, LEN, D), 1.0, 6.0, ((0, 4), (1, 8)))
    a_rows = draw_a_rows(jax.random.fold_in(streams_of[5], 71), 0)
    b_rows = centred(streams_of[3], (SECTIONS, RANK, D), (8 * RANK) ** -0.5, 0.375, ((0, 16), (2, 32)))
    gain = jnp.clip(1.0 + 0.1 * jax.random.normal(streams_of[4], (SECTIONS, D), jnp.float32), 0.5, 1.5).astype(jnp.bfloat16)
    return {"acts": acts, "top_grad": top_grad, "a_rows": a_rows, "b_rows": b_rows, "gain": gain}


def layer_back(upstream_gradient, pieces):
    hidden, a_full, b_full, gain_row = pieces
    hidden_float = hidden.astype(jnp.float32)
    inverse_root_mean = jnp.sqrt(lax.optimization_barrier(jnp.mean(hidden_float * hidden_float, axis=-1, keepdims=True)) + 1e-05)
    input_normalized = hidden_float / inverse_root_mean
    gain_float = gain_row.astype(jnp.float32)
    normalized_rows = (input_normalized * gain_float).astype(jnp.bfloat16)
    low = jnp.dot(normalized_rows, a_full.T, preferred_element_type=jnp.float32).astype(jnp.bfloat16)
    d_low = jnp.dot(upstream_gradient, b_full.T, preferred_element_type=jnp.float32).astype(jnp.bfloat16)
    normalized_gradient = jnp.dot(d_low, a_full, preferred_element_type=jnp.float32)
    input_gradient = normalized_gradient * gain_float
    hidden_gradient = upstream_gradient.astype(jnp.float32) + (input_gradient - input_normalized * lax.optimization_barrier(jnp.mean(input_gradient * input_normalized, axis=-1, keepdims=True))) / inverse_root_mean
    grad_a = jnp.dot(d_low.T, normalized_rows, preferred_element_type=jnp.float32)
    grad_b = jnp.dot(low.T, upstream_gradient, preferred_element_type=jnp.float32)
    gain_gradient = lax.optimization_barrier(jnp.sum(normalized_gradient * input_normalized, axis=0))
    return (hidden_gradient.astype(jnp.bfloat16), (grad_a, grad_b, gain_gradient))

def reference(acts, top_grad, a_rows, b_rows, gain):
    bound = math.sqrt(N_PIPE * (2 * RANK + 1) * D)
    total_a = jnp.zeros(a_rows.shape, jnp.float32)
    total_b = jnp.zeros(b_rows.shape, jnp.float32)
    total_g = jnp.zeros(gain.shape, jnp.float32)
    factors = []
    for example in range(N_DP):
        _, (grad_a, grad_b, gain_gradient) = lax.scan(layer_back, top_grad[example], (acts[:, example], a_rows, b_rows, gain), reverse=True)
        square = jnp.sum(grad_a * grad_a) + jnp.sum(grad_b * grad_b) + jnp.sum(gain_gradient * gain_gradient)
        factor = bound / (jnp.sqrt(square) + 0.01 * bound)
        total_a = total_a + factor * grad_a
        total_b = total_b + factor * grad_b
        total_g = total_g + factor * gain_gradient
        factors.append(factor)
    return (total_a, total_b, total_g, jnp.stack(factors).astype(jnp.float32))
```

```python
import math

import jax
import jax.numpy as jnp
from jax import lax
from jax.sharding import PartitionSpec as P

rows_per_block = 16


def from_behind(value, axis, steps):
    count = lax.axis_size(axis)
    initial, last = (max(0, -steps), min(count, count - steps))
    return lax.ppermute(value, axis, [(source, source + steps) for source in range(initial, last)])


def on_device(acts, top_grad, a_rows, b_rows, gain):
    sections = lax.axis_size("pipe")
    section = lax.axis_index("pipe")
    hidden = acts[0, 0]
    top = top_grad[0]
    rank = a_rows.shape[1]
    params = jnp.concatenate([a_rows[0], b_rows[0], gain], axis=0)
    whole = lax.all_gather(params, ("seq", "dp"), axis=1, tiled=True)
    a_full = whole[:rank]
    b_full = whole[rank : 2 * rank]
    gain_float = whole[2 * rank].astype(jnp.float32)
    rows, width = hidden.shape
    block_total = rows // rows_per_block
    hidden_float = hidden.astype(jnp.float32)
    inverse_root_mean = jnp.sqrt(
        jnp.mean(hidden_float * hidden_float, axis=-1, keepdims=True) + 1e-05
    )
    input_normalized = hidden_float / inverse_root_mean
    normalized_rows = (input_normalized * gain_float).astype(jnp.bfloat16)
    low = jnp.dot(normalized_rows, a_full.T, preferred_element_type=jnp.float32).astype(
        jnp.bfloat16
    )
    contract_last = (((1,), (1,)), ((), ()))
    contract_first = (((0,), (0,)), ((), ()))

    def back_block(upstream_gradient, block_offset):
        hidden_part = lax.dynamic_slice_in_dim(hidden, block_offset, rows_per_block, 0)
        r_part = lax.dynamic_slice_in_dim(inverse_root_mean, block_offset, rows_per_block, 0)
        input_portion = hidden_part.astype(jnp.float32) / r_part
        d_low = lax.dot_general(
            upstream_gradient, b_full, contract_last, preferred_element_type=jnp.float32
        ).astype(jnp.bfloat16)
        normalized_gradient = jnp.dot(d_low, a_full, preferred_element_type=jnp.float32)
        input_gradient = normalized_gradient * gain_float
        hidden_gradient = (
            upstream_gradient.astype(jnp.float32)
            + (
                input_gradient
                - input_portion * jnp.mean(input_gradient * input_portion, axis=-1, keepdims=True)
            )
            / r_part
        )
        return hidden_gradient.astype(jnp.bfloat16)

    def turn(turn_index, carry):
        incoming, store = carry
        block_index = turn_index - (sections - 1 - section)
        inside = jnp.logical_and(block_index >= 0, block_index < block_total)
        block_offset = jnp.clip(block_index, 0, block_total - 1) * rows_per_block
        top_block = lax.dynamic_slice_in_dim(top, block_offset, rows_per_block, 0)
        source = jnp.where(section == sections - 1, top_block, incoming)
        slot = jnp.where(inside, block_index, block_total)
        store = lax.dynamic_update_slice_in_dim(store, source[None], slot, 0)
        result = back_block(source, block_offset)
        incoming = from_behind(result, "pipe", -1)
        return (incoming, store)

    begin = (
        jnp.zeros((rows_per_block, width), jnp.bfloat16),
        jnp.zeros((block_total + 1, rows_per_block, width), jnp.bfloat16),
    )
    store = lax.fori_loop(0, sections + block_total - 1, turn, begin)[1]
    mine = store[:block_total].reshape(rows, width)
    d_low = lax.dot_general(mine, b_full, contract_last, preferred_element_type=jnp.float32).astype(
        jnp.bfloat16
    )
    normalized_gradient = jnp.dot(d_low, a_full, preferred_element_type=jnp.float32)
    grad_a = lax.dot_general(
        d_low, normalized_rows, contract_first, preferred_element_type=jnp.float32
    )
    grad_b = lax.dot_general(low, mine, contract_first, preferred_element_type=jnp.float32)
    gain_gradient = jnp.sum(normalized_gradient * input_normalized, axis=0)[None, :]
    grads = jnp.concatenate([grad_a, grad_b, gain_gradient], axis=0)
    part = lax.psum_scatter(grads, "seq", scatter_dimension=1, tiled=True)
    examples = lax.axis_size("dp")
    example = lax.axis_index("dp")
    square = jnp.sum(part * part)
    squares = jnp.where(jnp.arange(examples) == example, square, 0.0).astype(jnp.float32)
    totals = lax.psum(squares, ("pipe", "seq", "dp"))
    bound = math.sqrt(sections * (2 * rank + 1) * width)
    factors = bound / (jnp.sqrt(totals) + 0.01 * bound)
    gathered = lax.all_gather(part, "dp", axis=0, tiled=False)
    share = part.shape[1] // examples
    pieces = lax.dynamic_slice_in_dim(gathered, example * share, share, 2)
    combined = jnp.sum(factors[:, None, None] * pieces, axis=0)
    out_a = combined[:rank]
    out_b = combined[rank : 2 * rank]
    out_g = combined[2 * rank :]
    factor = lax.dynamic_slice_in_dim(factors, example, 1, 0)
    return (out_a[None], out_b[None], out_g, factor)


def solution(mesh):
    in_specs = (
        P("pipe", "dp", "seq", None),
        P("dp", "seq", None),
        P("pipe", None, ("seq", "dp")),
        P("pipe", None, ("seq", "dp")),
        P("pipe", ("seq", "dp")),
    )
    out_specs = (
        P("pipe", None, ("seq", "dp")),
        P("pipe", None, ("seq", "dp")),
        P("pipe", ("seq", "dp")),
        P("dp"),
    )
    return jax.shard_map(
        on_device, mesh=mesh, in_specs=in_specs, out_specs=out_specs, check_vma=False
    )
```

```python
import math

import jax
import jax.numpy as jnp
from jax import lax
from jax.sharding import PartitionSpec as P

rows_per_block = 16


def from_behind(value, axis, steps):
    count = lax.axis_size(axis)
    initial, last = (max(0, -steps), min(count, count - steps))
    return lax.ppermute(value, axis, [(source, source + steps) for source in range(initial, last)])


def on_device(acts, top_grad, a_rows, b_rows, gain):
    sections = lax.axis_size("pipe")
    section = lax.axis_index("pipe")
    hidden = acts[0, 0]
    top = top_grad[0]
    rank = a_rows.shape[1]
    params = jnp.concatenate([a_rows[0], b_rows[0], gain], axis=0)
    whole = lax.all_gather(lax.all_gather(params, "dp", axis=1, tiled=True), "seq", axis=1, tiled=True)
    a_full = whole[:rank]
    b_full = whole[rank : 2 * rank]
    gain_float = whole[2 * rank].astype(jnp.float32)
    rows, width = hidden.shape
    block_total = rows // rows_per_block
    hidden_float = hidden.astype(jnp.float32)
    inverse_root_mean = jnp.sqrt(
        jnp.mean(hidden_float * hidden_float, axis=-1, keepdims=True) + 1e-05
    )
    input_normalized = hidden_float / inverse_root_mean
    normalized_rows = (input_normalized * gain_float).astype(jnp.bfloat16)
    low = jnp.dot(normalized_rows, a_full.T, preferred_element_type=jnp.float32).astype(
        jnp.bfloat16
    )
    contract_last = (((1,), (1,)), ((), ()))
    contract_first = (((0,), (0,)), ((), ()))

    def back_block(upstream_gradient, block_offset):
        hidden_part = lax.dynamic_slice_in_dim(hidden, block_offset, rows_per_block, 0)
        r_part = lax.dynamic_slice_in_dim(inverse_root_mean, block_offset, rows_per_block, 0)
        input_portion = hidden_part.astype(jnp.float32) / r_part
        d_low = lax.dot_general(
            upstream_gradient, b_full, contract_last, preferred_element_type=jnp.float32
        ).astype(jnp.bfloat16)
        normalized_gradient = jnp.dot(d_low, a_full, preferred_element_type=jnp.float32)
        input_gradient = normalized_gradient * gain_float
        hidden_gradient = (
            upstream_gradient.astype(jnp.float32)
            + (
                input_gradient
                - input_portion * jnp.mean(input_gradient * input_portion, axis=-1, keepdims=True)
            )
            / r_part
        )
        return hidden_gradient.astype(jnp.bfloat16)

    def turn(turn_index, carry):
        incoming, store = carry
        block_index = turn_index - (sections - 1 - section)
        inside = jnp.logical_and(block_index >= 0, block_index < block_total)
        block_offset = jnp.clip(block_index, 0, block_total - 1) * rows_per_block
        top_block = lax.dynamic_slice_in_dim(top, block_offset, rows_per_block, 0)
        source = jnp.where(section == sections - 1, top_block, incoming)
        slot = jnp.where(inside, block_index, block_total)
        store = lax.dynamic_update_slice_in_dim(store, source[None], slot, 0)
        result = back_block(source, block_offset)
        incoming = from_behind(result, "pipe", -1)
        return (incoming, store)

    begin = (
        jnp.zeros((rows_per_block, width), jnp.bfloat16),
        jnp.zeros((block_total + 1, rows_per_block, width), jnp.bfloat16),
    )
    store = lax.fori_loop(0, sections + block_total - 1, turn, begin, unroll=True)[1]
    mine = store[:block_total].reshape(rows, width)
    d_low = lax.dot_general(mine, b_full, contract_last, preferred_element_type=jnp.float32).astype(
        jnp.bfloat16
    )
    normalized_gradient = jnp.dot(d_low, a_full, preferred_element_type=jnp.float32)
    grad_a = lax.dot_general(
        d_low, normalized_rows, contract_first, preferred_element_type=jnp.float32
    )
    grad_b = lax.dot_general(low, mine, contract_first, preferred_element_type=jnp.float32)
    gain_gradient = jnp.sum(normalized_gradient * input_normalized, axis=0)[None, :]
    grads = jnp.concatenate([grad_a, grad_b, gain_gradient], axis=0)
    part = lax.psum_scatter(grads, "seq", scatter_dimension=1, tiled=True)
    examples = lax.axis_size("dp")
    example = lax.axis_index("dp")
    square = jnp.sum(part * part)
    total = lax.psum(square, "pipe")
    count = lax.axis_size("seq")
    step = 1
    while step < count:
        total = total + lax.ppermute(
            total, "seq", [(source, (source + step) % count) for source in range(count)]
        )
        step *= 2
    bound = math.sqrt(sections * (2 * rank + 1) * width)
    factor = bound / (jnp.sqrt(total) + 0.01 * bound)
    scaled = factor * part
    share = part.shape[1] // examples
    combined = lax.dynamic_slice_in_dim(scaled, example * share, share, 1)
    for step in range(1, examples):
        target = lax.rem(example + step, examples)
        piece = lax.dynamic_slice_in_dim(scaled, target * share, share, 1)
        combined = combined + lax.ppermute(
            piece, "dp", [(source, (source + step) % examples) for source in range(examples)]
        )
    out_a = combined[:rank]
    out_b = combined[rank : 2 * rank]
    out_g = combined[2 * rank :]
    factor = jnp.reshape(factor, (1,))
    return (out_a[None], out_b[None], out_g, factor)


def solution(mesh):
    in_specs = (
        P("pipe", "dp", "seq", None),
        P("dp", "seq", None),
        P("pipe", None, ("seq", "dp")),
        P("pipe", None, ("seq", "dp")),
        P("pipe", ("seq", "dp")),
    )
    out_specs = (
        P("pipe", None, ("seq", "dp")),
        P("pipe", None, ("seq", "dp")),
        P("pipe", ("seq", "dp")),
        P("dp"),
    )
    return jax.shard_map(
        on_device, mesh=mesh, in_specs=in_specs, out_specs=out_specs, check_vma=False
    )
```

```python
import math

import jax
import jax.numpy as jnp
from jax import lax
from jax.sharding import PartitionSpec as P

rows_per_block = 16


def from_behind(value, axis, steps):
    count = lax.axis_size(axis)
    initial, last = (max(0, -steps), min(count, count - steps))
    return lax.ppermute(value, axis, [(source, source + steps) for source in range(initial, last)])


def on_device(acts, top_grad, a_rows, b_rows, gain):
    sections = lax.axis_size("pipe")
    section = lax.axis_index("pipe")
    hidden = acts[0, 0]
    top = top_grad[0]
    rank = a_rows.shape[1]
    params = jnp.concatenate([a_rows[0], b_rows[0], gain], axis=0)
    whole = lax.all_gather(lax.all_gather(params, "dp", axis=1, tiled=True), "seq", axis=1, tiled=True)
    a_full = whole[:rank]
    b_full = whole[rank : 2 * rank]
    gain_float = whole[2 * rank].astype(jnp.float32)
    rows, width = hidden.shape
    block_total = rows // rows_per_block
    hidden_float = hidden.astype(jnp.float32)
    inverse_root_mean = jnp.sqrt(
        jnp.mean(hidden_float * hidden_float, axis=-1, keepdims=True) + 1e-05
    )
    input_normalized = hidden_float / inverse_root_mean
    normalized_rows = (input_normalized * gain_float).astype(jnp.bfloat16)
    low = jnp.dot(normalized_rows, a_full.T, preferred_element_type=jnp.float32).astype(
        jnp.bfloat16
    )
    contract_last = (((1,), (1,)), ((), ()))
    contract_first = (((0,), (0,)), ((), ()))

    def turn(turn_index, carry):
        incoming, sum_a, sum_b, sum_g = carry
        block_index = turn_index - (sections - 1 - section)
        inside = jnp.logical_and(block_index >= 0, block_index < block_total)
        block_offset = jnp.clip(block_index, 0, block_total - 1) * rows_per_block
        top_block = lax.dynamic_slice_in_dim(top, block_offset, rows_per_block, 0)
        source = jnp.where(section == sections - 1, top_block, incoming)
        hidden_part = lax.dynamic_slice_in_dim(hidden, block_offset, rows_per_block, 0)
        r_part = lax.dynamic_slice_in_dim(inverse_root_mean, block_offset, rows_per_block, 0)
        input_portion = hidden_part.astype(jnp.float32) / r_part
        d_low = lax.dot_general(
            source, b_full, contract_last, preferred_element_type=jnp.float32
        ).astype(jnp.bfloat16)
        normalized_gradient = jnp.dot(d_low, a_full, preferred_element_type=jnp.float32)
        input_gradient = normalized_gradient * gain_float
        hidden_gradient = (
            source.astype(jnp.float32)
            + (
                input_gradient
                - input_portion * jnp.mean(input_gradient * input_portion, axis=-1, keepdims=True)
            )
            / r_part
        )
        incoming = from_behind(hidden_gradient.astype(jnp.bfloat16), "pipe", -1)
        normalized_part = (input_portion * gain_float).astype(jnp.bfloat16)
        low_part = lax.dynamic_slice_in_dim(low, block_offset, rows_per_block, 0)
        part_a = lax.dot_general(
            d_low, normalized_part, contract_first, preferred_element_type=jnp.float32
        )
        part_b = lax.dot_general(low_part, source, contract_first, preferred_element_type=jnp.float32)
        part_g = jnp.sum(normalized_gradient * input_portion, axis=0)[None, :]
        sum_a = sum_a + jnp.where(inside, part_a, 0.0)
        sum_b = sum_b + jnp.where(inside, part_b, 0.0)
        sum_g = sum_g + jnp.where(inside, part_g, 0.0)
        return (incoming, sum_a, sum_b, sum_g)

    begin = (
        jnp.zeros((rows_per_block, width), jnp.bfloat16),
        jnp.zeros((rank, width), jnp.float32),
        jnp.zeros((rank, width), jnp.float32),
        jnp.zeros((1, width), jnp.float32),
    )
    _, grad_a, grad_b, gain_gradient = lax.fori_loop(
        0, sections + block_total - 1, turn, begin
    )
    grads = jnp.concatenate([grad_a, grad_b, gain_gradient], axis=0)
    part = lax.psum_scatter(grads, "seq", scatter_dimension=1, tiled=True)
    examples = lax.axis_size("dp")
    example = lax.axis_index("dp")
    square = jnp.sum(part * part)
    total = lax.psum(square, "pipe")
    count = lax.axis_size("seq")
    step = 1
    while step < count:
        total = total + lax.ppermute(
            total, "seq", [(source, (source + step) % count) for source in range(count)]
        )
        step *= 2
    bound = math.sqrt(sections * (2 * rank + 1) * width)
    factor = bound / (jnp.sqrt(total) + 0.01 * bound)
    scaled = factor * part
    share = part.shape[1] // examples
    combined = lax.dynamic_slice_in_dim(scaled, example * share, share, 1)
    for step in range(1, examples):
        target = lax.rem(example + step, examples)
        piece = lax.dynamic_slice_in_dim(scaled, target * share, share, 1)
        combined = combined + lax.ppermute(
            piece, "dp", [(source, (source + step) % examples) for source in range(examples)]
        )
    out_a = combined[:rank]
    out_b = combined[rank : 2 * rank]
    out_g = combined[2 * rank :]
    factor = jnp.reshape(factor, (1,))
    return (out_a[None], out_b[None], out_g, factor)


def solution(mesh):
    in_specs = (
        P("pipe", "dp", "seq", None),
        P("dp", "seq", None),
        P("pipe", None, ("seq", "dp")),
        P("pipe", None, ("seq", "dp")),
        P("pipe", ("seq", "dp")),
    )
    out_specs = (
        P("pipe", None, ("seq", "dp")),
        P("pipe", None, ("seq", "dp")),
        P("pipe", ("seq", "dp")),
        P("dp"),
    )
    return jax.shard_map(
        on_device, mesh=mesh, in_specs=in_specs, out_specs=out_specs, check_vma=False
    )
```

```python
import math

import jax
import jax.numpy as jnp
from jax import lax
from jax.sharding import PartitionSpec as P

rows_per_block = 16


def shifted(value, axis, steps):
    count = lax.axis_size(axis)
    initial, last = (max(0, -steps), min(count, count - steps))
    return lax.ppermute(value, axis, [(source, source + steps) for source in range(initial, last)])


def partner_swap(value, axis):
    count = lax.axis_size(axis)
    return lax.ppermute(value, axis, [(source, source ^ 1) for source in range(count)])


def on_device(acts, top_grad, a_rows, b_rows, gain):
    sections = lax.axis_size("pipe")
    section = lax.axis_index("pipe")
    pairs = sections // 2
    pair = section // 2
    upper_half = section % 2 == 1
    rank = a_rows.shape[1]
    own_hidden = acts[0, 0]
    rows, width = own_hidden.shape
    half_rows = rows // 2
    my_offset = jnp.where(upper_half, 0, half_rows)
    other_offset = half_rows - my_offset
    own_mine = lax.dynamic_slice_in_dim(own_hidden, my_offset, half_rows, 0)
    partner_rows = partner_swap(lax.dynamic_slice_in_dim(own_hidden, other_offset, half_rows, 0), "pipe")
    hidden_pair = (
        jnp.where(upper_half, own_mine, partner_rows),
        jnp.where(upper_half, partner_rows, own_mine),
    )
    top = lax.dynamic_slice_in_dim(top_grad[0], my_offset, half_rows, 0)
    params = jnp.concatenate([a_rows[0], b_rows[0], gain], axis=0)
    partner_params = partner_swap(params, "pipe")
    stacked = jnp.stack(
        [jnp.where(upper_half, params, partner_params), jnp.where(upper_half, partner_params, params)]
    )
    whole = lax.all_gather(lax.all_gather(stacked, "dp", axis=2, tiled=True), "seq", axis=2, tiled=True)
    contract_last = (((1,), (1,)), ((), ()))
    contract_first = (((0,), (0,)), ((), ()))
    layers = []
    for index in range(2):
        hidden = hidden_pair[index]
        a_full = whole[index, :rank]
        b_full = whole[index, rank : 2 * rank]
        gain_float = whole[index, 2 * rank].astype(jnp.float32)
        hidden_float = hidden.astype(jnp.float32)
        inverse_root_mean = jnp.sqrt(
            jnp.mean(hidden_float * hidden_float, axis=-1, keepdims=True) + 1e-05
        )
        normalized_rows = ((hidden_float / inverse_root_mean) * gain_float).astype(jnp.bfloat16)
        low = jnp.dot(normalized_rows, a_full.T, preferred_element_type=jnp.float32).astype(
            jnp.bfloat16
        )
        layers.append((hidden, inverse_root_mean, low, a_full, b_full, gain_float))
    block_total = half_rows // rows_per_block

    def layer_block(layer, source, block_offset, sums, inside):
        hidden, inverse_root_mean, low, a_full, b_full, gain_float = layer
        sum_a, sum_b, sum_g = sums
        hidden_part = lax.dynamic_slice_in_dim(hidden, block_offset, rows_per_block, 0)
        r_part = lax.dynamic_slice_in_dim(inverse_root_mean, block_offset, rows_per_block, 0)
        input_portion = hidden_part.astype(jnp.float32) / r_part
        d_low = lax.dot_general(
            source, b_full, contract_last, preferred_element_type=jnp.float32
        ).astype(jnp.bfloat16)
        normalized_gradient = jnp.dot(d_low, a_full, preferred_element_type=jnp.float32)
        input_gradient = normalized_gradient * gain_float
        hidden_gradient = (
            source.astype(jnp.float32)
            + (
                input_gradient
                - input_portion * jnp.mean(input_gradient * input_portion, axis=-1, keepdims=True)
            )
            / r_part
        ).astype(jnp.bfloat16)
        normalized_part = (input_portion * gain_float).astype(jnp.bfloat16)
        low_part = lax.dynamic_slice_in_dim(low, block_offset, rows_per_block, 0)
        part_a = lax.dot_general(
            d_low, normalized_part, contract_first, preferred_element_type=jnp.float32
        )
        part_b = lax.dot_general(low_part, source, contract_first, preferred_element_type=jnp.float32)
        part_g = jnp.sum(normalized_gradient * input_portion, axis=0)[None, :]
        sums = (
            sum_a + jnp.where(inside, part_a, 0.0),
            sum_b + jnp.where(inside, part_b, 0.0),
            sum_g + jnp.where(inside, part_g, 0.0),
        )
        return hidden_gradient, sums

    def turn(turn_index, carry):
        incoming, upper_sums, lower_sums = carry
        block_index = turn_index - (pairs - 1 - pair)
        inside = jnp.logical_and(block_index >= 0, block_index < block_total)
        block_offset = jnp.clip(block_index, 0, block_total - 1) * rows_per_block
        top_block = lax.dynamic_slice_in_dim(top, block_offset, rows_per_block, 0)
        source = jnp.where(pair == pairs - 1, top_block, incoming)
        middle, upper_sums = layer_block(layers[0], source, block_offset, upper_sums, inside)
        result, lower_sums = layer_block(layers[1], middle, block_offset, lower_sums, inside)
        incoming = shifted(result, "pipe", -2)
        return (incoming, upper_sums, lower_sums)

    def zero_sums():
        return (
            jnp.zeros((rank, width), jnp.float32),
            jnp.zeros((rank, width), jnp.float32),
            jnp.zeros((1, width), jnp.float32),
        )

    begin = (jnp.zeros((rows_per_block, width), jnp.bfloat16), zero_sums(), zero_sums())
    _, upper_sums, lower_sums = lax.fori_loop(0, pairs + block_total - 1, turn, begin)
    grads = jnp.stack(
        [jnp.concatenate(upper_sums, axis=0), jnp.concatenate(lower_sums, axis=0)]
    )
    reduced = lax.psum_scatter(grads, "seq", scatter_dimension=2, tiled=True)
    own_layer = jnp.where(upper_half, reduced[0], reduced[1])
    other_layer = jnp.where(upper_half, reduced[1], reduced[0])
    part = own_layer + partner_swap(other_layer, "pipe")
    examples = lax.axis_size("dp")
    example = lax.axis_index("dp")
    square = jnp.sum(part * part)
    total = lax.psum(square, "pipe")
    count = lax.axis_size("seq")
    step = 1
    while step < count:
        total = total + lax.ppermute(
            total, "seq", [(source, (source + step) % count) for source in range(count)]
        )
        step *= 2
    bound = math.sqrt(sections * (2 * rank + 1) * width)
    factor = bound / (jnp.sqrt(total) + 0.01 * bound)
    scaled = factor * part
    share = part.shape[1] // examples
    combined = lax.dynamic_slice_in_dim(scaled, example * share, share, 1)
    for step in range(1, examples):
        target = lax.rem(example + step, examples)
        piece = lax.dynamic_slice_in_dim(scaled, target * share, share, 1)
        combined = combined + lax.ppermute(
            piece, "dp", [(source, (source + step) % examples) for source in range(examples)]
        )
    out_a = combined[:rank]
    out_b = combined[rank : 2 * rank]
    out_g = combined[2 * rank :]
    factor = jnp.reshape(factor, (1,))
    return (out_a[None], out_b[None], out_g, factor)


def solution(mesh):
    in_specs = (
        P("pipe", "dp", "seq", None),
        P("dp", "seq", None),
        P("pipe", None, ("seq", "dp")),
        P("pipe", None, ("seq", "dp")),
        P("pipe", ("seq", "dp")),
    )
    out_specs = (
        P("pipe", None, ("seq", "dp")),
        P("pipe", None, ("seq", "dp")),
        P("pipe", ("seq", "dp")),
        P("dp"),
    )
    return jax.shard_map(
        on_device, mesh=mesh, in_specs=in_specs, out_specs=out_specs, check_vma=False
    )
```

```python
import math

import jax
import jax.numpy as jnp
from jax import lax
from jax.sharding import PartitionSpec as P

rows_per_block = 16


def shifted(value, axis, steps):
    count = lax.axis_size(axis)
    initial, last = (max(0, -steps), min(count, count - steps))
    return lax.ppermute(value, axis, [(source, source + steps) for source in range(initial, last)])


def partner_swap(value, axis):
    count = lax.axis_size(axis)
    return lax.ppermute(value, axis, [(source, source ^ 1) for source in range(count)])


def on_device(acts, top_grad, a_rows, b_rows, gain):
    sections = lax.axis_size("pipe")
    section = lax.axis_index("pipe")
    pairs = sections // 2
    pair = section // 2
    upper_half = section % 2 == 1
    rank = a_rows.shape[1]
    own_hidden = acts[0, 0]
    rows, width = own_hidden.shape
    half_rows = rows // 2
    my_offset = jnp.where(upper_half, 0, half_rows)
    other_offset = half_rows - my_offset
    own_mine = lax.dynamic_slice_in_dim(own_hidden, my_offset, half_rows, 0)
    partner_rows = partner_swap(lax.dynamic_slice_in_dim(own_hidden, other_offset, half_rows, 0), "pipe")
    hidden_pair = (
        jnp.where(upper_half, own_mine, partner_rows),
        jnp.where(upper_half, partner_rows, own_mine),
    )
    top = lax.dynamic_slice_in_dim(top_grad[0], my_offset, half_rows, 0)
    params = jnp.concatenate([a_rows[0], b_rows[0], gain], axis=0)
    partner_params = partner_swap(params, "pipe")
    stacked = jnp.stack(
        [jnp.where(upper_half, params, partner_params), jnp.where(upper_half, partner_params, params)]
    )
    whole = lax.all_gather(lax.all_gather(stacked, "dp", axis=2, tiled=True), "seq", axis=2, tiled=True)
    contract_last = (((1,), (1,)), ((), ()))
    contract_first = (((0,), (0,)), ((), ()))
    layers = []
    for index in range(2):
        hidden = hidden_pair[index]
        a_full = whole[index, :rank]
        b_full = whole[index, rank : 2 * rank]
        gain_float = whole[index, 2 * rank].astype(jnp.float32)
        hidden_float = hidden.astype(jnp.float32)
        inverse_root_mean = jnp.sqrt(
            jnp.mean(hidden_float * hidden_float, axis=-1, keepdims=True) + 1e-05
        )
        normalized_rows = ((hidden_float / inverse_root_mean) * gain_float).astype(jnp.bfloat16)
        low = jnp.dot(normalized_rows, a_full.T, preferred_element_type=jnp.float32).astype(
            jnp.bfloat16
        )
        layers.append((hidden, inverse_root_mean, low, a_full, b_full, gain_float))
    block_total = half_rows // rows_per_block

    def layer_block(layer, source, block_offset):
        hidden, inverse_root_mean, low, a_full, b_full, gain_float = layer
        hidden_part = lax.dynamic_slice_in_dim(hidden, block_offset, rows_per_block, 0)
        r_part = lax.dynamic_slice_in_dim(inverse_root_mean, block_offset, rows_per_block, 0)
        input_portion = hidden_part.astype(jnp.float32) / r_part
        d_low = lax.dot_general(
            source, b_full, contract_last, preferred_element_type=jnp.float32
        ).astype(jnp.bfloat16)
        normalized_gradient = jnp.dot(d_low, a_full, preferred_element_type=jnp.float32)
        input_gradient = normalized_gradient * gain_float
        hidden_gradient = (
            source.astype(jnp.float32)
            + (
                input_gradient
                - input_portion * jnp.mean(input_gradient * input_portion, axis=-1, keepdims=True)
            )
            / r_part
        ).astype(jnp.bfloat16)
        return hidden_gradient

    def turn(turn_index, carry):
        incoming, upper_store, lower_store = carry
        block_index = turn_index - (pairs - 1 - pair)
        inside = jnp.logical_and(block_index >= 0, block_index < block_total)
        block_offset = jnp.clip(block_index, 0, block_total - 1) * rows_per_block
        top_block = lax.dynamic_slice_in_dim(top, block_offset, rows_per_block, 0)
        source = jnp.where(pair == pairs - 1, top_block, incoming)
        middle = layer_block(layers[0], source, block_offset)
        result = layer_block(layers[1], middle, block_offset)
        incoming = shifted(result, "pipe", -2)
        slot = jnp.where(inside, block_index, block_total)
        upper_store = lax.dynamic_update_slice_in_dim(upper_store, source[None], slot, 0)
        lower_store = lax.dynamic_update_slice_in_dim(lower_store, middle[None], slot, 0)
        return (incoming, upper_store, lower_store)

    store = jnp.zeros((block_total + 1, rows_per_block, width), jnp.bfloat16)
    begin = (jnp.zeros((rows_per_block, width), jnp.bfloat16), store, store)
    _, upper_store, lower_store = lax.fori_loop(0, pairs + block_total - 1, turn, begin)
    per_layer = []
    for layer, stored in zip(layers, (upper_store, lower_store)):
        hidden, inverse_root_mean, low, a_full, b_full, gain_float = layer
        mine = stored[:block_total].reshape(half_rows, width)
        input_normalized = hidden.astype(jnp.float32) / inverse_root_mean
        normalized_rows = (input_normalized * gain_float).astype(jnp.bfloat16)
        d_low = lax.dot_general(
            mine, b_full, contract_last, preferred_element_type=jnp.float32
        ).astype(jnp.bfloat16)
        normalized_gradient = jnp.dot(d_low, a_full, preferred_element_type=jnp.float32)
        grad_a = lax.dot_general(
            d_low, normalized_rows, contract_first, preferred_element_type=jnp.float32
        )
        grad_b = lax.dot_general(low, mine, contract_first, preferred_element_type=jnp.float32)
        gain_gradient = jnp.sum(normalized_gradient * input_normalized, axis=0)[None, :]
        per_layer.append(jnp.concatenate([grad_a, grad_b, gain_gradient], axis=0))
    grads = jnp.stack(per_layer).astype(jnp.bfloat16)
    reduced = lax.psum_scatter(grads, "seq", scatter_dimension=2, tiled=True).astype(jnp.float32)
    own_layer = jnp.where(upper_half, reduced[0], reduced[1])
    other_layer = jnp.where(upper_half, reduced[1], reduced[0])
    part = own_layer + partner_swap(other_layer, "pipe")
    examples = lax.axis_size("dp")
    example = lax.axis_index("dp")
    square = jnp.sum(part * part)
    total = lax.psum(square, "pipe")
    count = lax.axis_size("seq")
    step = 1
    while step < count:
        total = total + lax.ppermute(
            total, "seq", [(source, (source + step) % count) for source in range(count)]
        )
        step *= 2
    bound = math.sqrt(sections * (2 * rank + 1) * width)
    factor = bound / (jnp.sqrt(total) + 0.01 * bound)
    scaled = factor * part
    share = part.shape[1] // examples
    combined = lax.dynamic_slice_in_dim(scaled, example * share, share, 1)
    for step in range(1, examples):
        target = lax.rem(example + step, examples)
        piece = lax.dynamic_slice_in_dim(scaled, target * share, share, 1)
        combined = combined + lax.ppermute(
            piece, "dp", [(source, (source + step) % examples) for source in range(examples)]
        )
    out_a = combined[:rank]
    out_b = combined[rank : 2 * rank]
    out_g = combined[2 * rank :]
    factor = jnp.reshape(factor, (1,))
    return (out_a[None], out_b[None], out_g, factor)


def solution(mesh):
    in_specs = (
        P("pipe", "dp", "seq", None),
        P("dp", "seq", None),
        P("pipe", None, ("seq", "dp")),
        P("pipe", None, ("seq", "dp")),
        P("pipe", ("seq", "dp")),
    )
    out_specs = (
        P("pipe", None, ("seq", "dp")),
        P("pipe", None, ("seq", "dp")),
        P("pipe", ("seq", "dp")),
        P("dp"),
    )
    return jax.shard_map(
        on_device, mesh=mesh, in_specs=in_specs, out_specs=out_specs, check_vma=False
    )
```

```python
import math

import jax
import jax.numpy as jnp
from jax import lax
from jax.sharding import PartitionSpec as P

rows_per_block = 8


def shifted(value, axis, steps):
    count = lax.axis_size(axis)
    initial, last = (max(0, -steps), min(count, count - steps))
    return lax.ppermute(value, axis, [(source, source + steps) for source in range(initial, last)])


def partner_swap(value, axis):
    count = lax.axis_size(axis)
    return lax.ppermute(value, axis, [(source, source ^ 1) for source in range(count)])


def on_device(acts, top_grad, a_rows, b_rows, gain):
    sections = lax.axis_size("pipe")
    section = lax.axis_index("pipe")
    pairs = sections // 2
    pair = section // 2
    upper_half = section % 2 == 1
    rank = a_rows.shape[1]
    own_hidden = acts[0, 0]
    rows, width = own_hidden.shape
    half_rows = rows // 2
    my_offset = jnp.where(upper_half, 0, half_rows)
    other_offset = half_rows - my_offset
    own_mine = lax.dynamic_slice_in_dim(own_hidden, my_offset, half_rows, 0)
    partner_rows = partner_swap(lax.dynamic_slice_in_dim(own_hidden, other_offset, half_rows, 0), "pipe")
    hidden_pair = (
        jnp.where(upper_half, own_mine, partner_rows),
        jnp.where(upper_half, partner_rows, own_mine),
    )
    top = lax.dynamic_slice_in_dim(top_grad[0], my_offset, half_rows, 0)
    params = jnp.concatenate([a_rows[0], b_rows[0], gain], axis=0)
    partner_params = partner_swap(params, "pipe")
    stacked = jnp.stack(
        [jnp.where(upper_half, params, partner_params), jnp.where(upper_half, partner_params, params)]
    )
    whole = lax.all_gather(lax.all_gather(stacked, "dp", axis=2, tiled=True), "seq", axis=2, tiled=True)
    contract_last = (((1,), (1,)), ((), ()))
    contract_first = (((0,), (0,)), ((), ()))
    layers = []
    for index in range(2):
        hidden = hidden_pair[index]
        a_full = whole[index, :rank]
        b_full = whole[index, rank : 2 * rank]
        gain_float = whole[index, 2 * rank].astype(jnp.float32)
        hidden_float = hidden.astype(jnp.float32)
        inverse_root_mean = jnp.sqrt(
            jnp.mean(hidden_float * hidden_float, axis=-1, keepdims=True) + 1e-05
        )
        normalized_rows = ((hidden_float / inverse_root_mean) * gain_float).astype(jnp.bfloat16)
        low = jnp.dot(normalized_rows, a_full.T, preferred_element_type=jnp.float32).astype(
            jnp.bfloat16
        )
        layers.append((hidden, inverse_root_mean, low, a_full, b_full, gain_float))
    block_total = half_rows // rows_per_block

    def layer_block(layer, source, block_offset, sums, inside):
        hidden, inverse_root_mean, low, a_full, b_full, gain_float = layer
        sum_a, sum_b, sum_g = sums
        hidden_part = lax.dynamic_slice_in_dim(hidden, block_offset, rows_per_block, 0)
        r_part = lax.dynamic_slice_in_dim(inverse_root_mean, block_offset, rows_per_block, 0)
        input_portion = hidden_part.astype(jnp.float32) / r_part
        d_low = lax.dot_general(
            source, b_full, contract_last, preferred_element_type=jnp.float32
        ).astype(jnp.bfloat16)
        normalized_gradient = jnp.dot(d_low, a_full, preferred_element_type=jnp.float32)
        input_gradient = normalized_gradient * gain_float
        hidden_gradient = (
            source.astype(jnp.float32)
            + (
                input_gradient
                - input_portion * jnp.mean(input_gradient * input_portion, axis=-1, keepdims=True)
            )
            / r_part
        ).astype(jnp.bfloat16)
        normalized_part = (input_portion * gain_float).astype(jnp.bfloat16)
        low_part = lax.dynamic_slice_in_dim(low, block_offset, rows_per_block, 0)
        part_a = lax.dot_general(
            d_low, normalized_part, contract_first, preferred_element_type=jnp.float32
        )
        part_b = lax.dot_general(low_part, source, contract_first, preferred_element_type=jnp.float32)
        part_g = jnp.sum(normalized_gradient * input_portion, axis=0)[None, :]
        sums = (
            sum_a + jnp.where(inside, part_a, 0.0),
            sum_b + jnp.where(inside, part_b, 0.0),
            sum_g + jnp.where(inside, part_g, 0.0),
        )
        return hidden_gradient, sums

    def turn(turn_index, carry):
        incoming, upper_sums, lower_sums = carry
        block_index = turn_index - (pairs - 1 - pair)
        inside = jnp.logical_and(block_index >= 0, block_index < block_total)
        block_offset = jnp.clip(block_index, 0, block_total - 1) * rows_per_block
        top_block = lax.dynamic_slice_in_dim(top, block_offset, rows_per_block, 0)
        source = jnp.where(pair == pairs - 1, top_block, incoming)
        middle, upper_sums = layer_block(layers[0], source, block_offset, upper_sums, inside)
        result, lower_sums = layer_block(layers[1], middle, block_offset, lower_sums, inside)
        incoming = shifted(result, "pipe", -2)
        return (incoming, upper_sums, lower_sums)

    def zero_sums():
        return (
            jnp.zeros((rank, width), jnp.float32),
            jnp.zeros((rank, width), jnp.float32),
            jnp.zeros((1, width), jnp.float32),
        )

    begin = (jnp.zeros((rows_per_block, width), jnp.bfloat16), zero_sums(), zero_sums())
    _, upper_sums, lower_sums = lax.fori_loop(0, pairs + block_total - 1, turn, begin)
    grads = jnp.stack(
        [jnp.concatenate(upper_sums, axis=0), jnp.concatenate(lower_sums, axis=0)]
    )
    reduced = lax.psum_scatter(grads, "seq", scatter_dimension=2, tiled=True)
    own_layer = jnp.where(upper_half, reduced[0], reduced[1])
    other_layer = jnp.where(upper_half, reduced[1], reduced[0])
    part = own_layer + partner_swap(other_layer, "pipe")
    examples = lax.axis_size("dp")
    example = lax.axis_index("dp")
    square = jnp.sum(part * part)
    total = lax.psum(square, "pipe")
    count = lax.axis_size("seq")
    step = 1
    while step < count:
        total = total + lax.ppermute(
            total, "seq", [(source, (source + step) % count) for source in range(count)]
        )
        step *= 2
    bound = math.sqrt(sections * (2 * rank + 1) * width)
    factor = bound / (jnp.sqrt(total) + 0.01 * bound)
    scaled = factor * part
    share = part.shape[1] // examples
    combined = lax.dynamic_slice_in_dim(scaled, example * share, share, 1)
    for step in range(1, examples):
        target = lax.rem(example + step, examples)
        piece = lax.dynamic_slice_in_dim(scaled, target * share, share, 1)
        combined = combined + lax.ppermute(
            piece, "dp", [(source, (source + step) % examples) for source in range(examples)]
        )
    out_a = combined[:rank]
    out_b = combined[rank : 2 * rank]
    out_g = combined[2 * rank :]
    factor = jnp.reshape(factor, (1,))
    return (out_a[None], out_b[None], out_g, factor)


def solution(mesh):
    in_specs = (
        P("pipe", "dp", "seq", None),
        P("dp", "seq", None),
        P("pipe", None, ("seq", "dp")),
        P("pipe", None, ("seq", "dp")),
        P("pipe", ("seq", "dp")),
    )
    out_specs = (
        P("pipe", None, ("seq", "dp")),
        P("pipe", None, ("seq", "dp")),
        P("pipe", ("seq", "dp")),
        P("dp"),
    )
    return jax.shard_map(
        on_device, mesh=mesh, in_specs=in_specs, out_specs=out_specs, check_vma=False
    )
```

```python
import math

import jax
import jax.numpy as jnp
from jax import lax
from jax.experimental import pallas as pl
from jax.experimental.pallas import tpu as pltpu
from jax.sharding import PartitionSpec as P

rows_per_block = 16


def shifted(value, axis, steps):
    count = lax.axis_size(axis)
    initial, last = (max(0, -steps), min(count, count - steps))
    return lax.ppermute(value, axis, [(source, source + steps) for source in range(initial, last)])


def partner_swap(value, axis):
    count = lax.axis_size(axis)
    return lax.ppermute(value, axis, [(source, source ^ 1) for source in range(count)])


def chain_kernel(flags, top_ref, incoming_ref, *refs):
    (hidden_u, root_u, b_u, a_u, g_u, hidden_l, root_l, b_l, a_l, g_l,
     source_ref, middle_ref, result_ref, low_u_ref, low_l_ref, pg_u_ref, pg_l_ref) = refs
    source = jnp.where(flags[1] == 1, top_ref[...], incoming_ref[...])
    source_ref[...] = source

    def one_layer(upstream, hidden_ref, root_ref, b_ref, a_ref, g_ref, low_ref, pg_ref):
        root = root_ref[...]
        normalized = hidden_ref[...].astype(jnp.float32) / root
        d_low = lax.dot_general(
            upstream, b_ref[...], (((1,), (1,)), ((), ())), preferred_element_type=jnp.float32
        ).astype(jnp.bfloat16)
        normalized_gradient = jnp.dot(d_low, a_ref[...], preferred_element_type=jnp.float32)
        input_gradient = normalized_gradient * g_ref[...]
        mean = jnp.mean(input_gradient * normalized, axis=-1, keepdims=True)
        low_ref[...] = d_low
        pg_ref[...] = jnp.sum(normalized_gradient * normalized, axis=0, keepdims=True)
        return (upstream.astype(jnp.float32) + (input_gradient - normalized * mean) / root).astype(
            jnp.bfloat16
        )

    middle = one_layer(source, hidden_u, root_u, b_u, a_u, g_u, low_u_ref, pg_u_ref)
    middle_ref[...] = middle
    result_ref[...] = one_layer(middle, hidden_l, root_l, b_l, a_l, g_l, low_l_ref, pg_l_ref)


def chain_step(flags, top, incoming, upper, lower, rows):
    width = incoming.shape[1]
    rank = upper[2].shape[0]
    whole = lambda shape: pl.BlockSpec(shape, lambda i, f: (0, 0))
    block = lambda last: pl.BlockSpec((rows, last), lambda i, f: (f[0], 0))
    layer_specs = [block(width), block(1), whole((rank, width)), whole((rank, width)), whole((1, width))]
    out_shape = [
        jax.ShapeDtypeStruct((rows, width), jnp.bfloat16),
        jax.ShapeDtypeStruct((rows, width), jnp.bfloat16),
        jax.ShapeDtypeStruct((rows, width), jnp.bfloat16),
        jax.ShapeDtypeStruct((rows, rank), jnp.bfloat16),
        jax.ShapeDtypeStruct((rows, rank), jnp.bfloat16),
        jax.ShapeDtypeStruct((1, width), jnp.float32),
        jax.ShapeDtypeStruct((1, width), jnp.float32),
    ]
    out_specs = [whole((rows, width))] * 3 + [whole((rows, rank))] * 2 + [whole((1, width))] * 2
    return pl.pallas_call(
        chain_kernel,
        out_shape=out_shape,
        grid_spec=pltpu.PrefetchScalarGridSpec(
            num_scalar_prefetch=1,
            grid=(1,),
            in_specs=[block(width), whole((rows, width))] + layer_specs + layer_specs,
            out_specs=out_specs,
        ),
        cost_estimate=pl.CostEstimate(
            flops=8 * rows * width * rank, transcendentals=0, bytes_accessed=4 * rank * width * 2 + 12 * rows * width
        ),
    )(flags, top, incoming, *upper, *lower)


def on_device(acts, top_grad, a_rows, b_rows, gain):
    sections = lax.axis_size("pipe")
    section = lax.axis_index("pipe")
    pairs = sections // 2
    pair = section // 2
    upper_half = section % 2 == 1
    rank = a_rows.shape[1]
    own_hidden = acts[0, 0]
    rows, width = own_hidden.shape
    half_rows = rows // 2
    my_offset = jnp.where(upper_half, 0, half_rows)
    other_offset = half_rows - my_offset
    own_mine = lax.dynamic_slice_in_dim(own_hidden, my_offset, half_rows, 0)
    partner_rows = partner_swap(lax.dynamic_slice_in_dim(own_hidden, other_offset, half_rows, 0), "pipe")
    hidden_pair = (
        jnp.where(upper_half, own_mine, partner_rows),
        jnp.where(upper_half, partner_rows, own_mine),
    )
    top = lax.dynamic_slice_in_dim(top_grad[0], my_offset, half_rows, 0)
    params = jnp.concatenate([a_rows[0], b_rows[0], gain], axis=0)
    partner_params = partner_swap(params, "pipe")
    stacked = jnp.stack(
        [jnp.where(upper_half, params, partner_params), jnp.where(upper_half, partner_params, params)]
    )
    whole = lax.all_gather(lax.all_gather(stacked, "dp", axis=2, tiled=True), "seq", axis=2, tiled=True)
    contract_last = (((1,), (1,)), ((), ()))
    contract_first = (((0,), (0,)), ((), ()))
    layers = []
    operands = []
    for index in range(2):
        hidden = hidden_pair[index]
        a_full = whole[index, :rank]
        b_full = whole[index, rank : 2 * rank]
        gain_float = whole[index, 2 * rank].astype(jnp.float32)
        hidden_float = hidden.astype(jnp.float32)
        inverse_root_mean = jnp.sqrt(
            jnp.mean(hidden_float * hidden_float, axis=-1, keepdims=True) + 1e-05
        )
        normalized_rows = ((hidden_float / inverse_root_mean) * gain_float).astype(jnp.bfloat16)
        low = jnp.dot(normalized_rows, a_full.T, preferred_element_type=jnp.float32).astype(
            jnp.bfloat16
        )
        layers.append((hidden, inverse_root_mean, low, a_full, b_full, gain_float))
        operands.append((hidden, inverse_root_mean, b_full, a_full, gain_float[None, :]))
    block_total = half_rows // rows_per_block

    def accumulate(layer, source, d_low, part_g, block_offset, sums, inside):
        hidden, inverse_root_mean, low, a_full, b_full, gain_float = layer
        sum_a, sum_b, sum_g = sums
        hidden_part = lax.dynamic_slice_in_dim(hidden, block_offset, rows_per_block, 0)
        r_part = lax.dynamic_slice_in_dim(inverse_root_mean, block_offset, rows_per_block, 0)
        normalized_part = ((hidden_part.astype(jnp.float32) / r_part) * gain_float).astype(jnp.bfloat16)
        low_part = lax.dynamic_slice_in_dim(low, block_offset, rows_per_block, 0)
        part_a = lax.dot_general(
            d_low, normalized_part, contract_first, preferred_element_type=jnp.float32
        )
        part_b = lax.dot_general(low_part, source, contract_first, preferred_element_type=jnp.float32)
        return (
            sum_a + jnp.where(inside, part_a, 0.0),
            sum_b + jnp.where(inside, part_b, 0.0),
            sum_g + jnp.where(inside, part_g, 0.0),
        )

    def turn(turn_index, carry):
        incoming, upper_sums, lower_sums = carry
        block_index = turn_index - (pairs - 1 - pair)
        inside = jnp.logical_and(block_index >= 0, block_index < block_total)
        clipped = jnp.clip(block_index, 0, block_total - 1)
        block_offset = clipped * rows_per_block
        flags = jnp.stack([clipped, (pair == pairs - 1).astype(jnp.int32)]).astype(jnp.int32)
        source, middle, result, low_u, low_l, pg_u, pg_l = chain_step(
            flags, top, incoming, operands[0], operands[1], rows_per_block
        )
        incoming = shifted(result, "pipe", -2)
        upper_sums = accumulate(layers[0], source, low_u, pg_u, block_offset, upper_sums, inside)
        lower_sums = accumulate(layers[1], middle, low_l, pg_l, block_offset, lower_sums, inside)
        return (incoming, upper_sums, lower_sums)

    def zero_sums():
        return (
            jnp.zeros((rank, width), jnp.float32),
            jnp.zeros((rank, width), jnp.float32),
            jnp.zeros((1, width), jnp.float32),
        )

    begin = (jnp.zeros((rows_per_block, width), jnp.bfloat16), zero_sums(), zero_sums())
    _, upper_sums, lower_sums = lax.fori_loop(0, pairs + block_total - 1, turn, begin)
    grads = jnp.stack(
        [jnp.concatenate(upper_sums, axis=0), jnp.concatenate(lower_sums, axis=0)]
    )
    reduced = lax.psum_scatter(grads, "seq", scatter_dimension=2, tiled=True)
    own_layer = jnp.where(upper_half, reduced[0], reduced[1])
    other_layer = jnp.where(upper_half, reduced[1], reduced[0])
    part = own_layer + partner_swap(other_layer, "pipe")
    examples = lax.axis_size("dp")
    example = lax.axis_index("dp")
    square = jnp.sum(part * part)
    total = lax.psum(square, "pipe")
    count = lax.axis_size("seq")
    step = 1
    while step < count:
        total = total + lax.ppermute(
            total, "seq", [(source, (source + step) % count) for source in range(count)]
        )
        step *= 2
    bound = math.sqrt(sections * (2 * rank + 1) * width)
    factor = bound / (jnp.sqrt(total) + 0.01 * bound)
    scaled = factor * part
    share = part.shape[1] // examples
    combined = lax.dynamic_slice_in_dim(scaled, example * share, share, 1)
    for step in range(1, examples):
        target = lax.rem(example + step, examples)
        piece = lax.dynamic_slice_in_dim(scaled, target * share, share, 1)
        combined = combined + lax.ppermute(
            piece, "dp", [(source, (source + step) % examples) for source in range(examples)]
        )
    out_a = combined[:rank]
    out_b = combined[rank : 2 * rank]
    out_g = combined[2 * rank :]
    factor = jnp.reshape(factor, (1,))
    return (out_a[None], out_b[None], out_g, factor)


def solution(mesh):
    in_specs = (
        P("pipe", "dp", "seq", None),
        P("dp", "seq", None),
        P("pipe", None, ("seq", "dp")),
        P("pipe", None, ("seq", "dp")),
        P("pipe", ("seq", "dp")),
    )
    out_specs = (
        P("pipe", None, ("seq", "dp")),
        P("pipe", None, ("seq", "dp")),
        P("pipe", ("seq", "dp")),
        P("dp"),
    )
    return jax.shard_map(
        on_device, mesh=mesh, in_specs=in_specs, out_specs=out_specs, check_vma=False
    )
```

```python
import math

import jax
import jax.numpy as jnp
from jax import lax
from jax.experimental import pallas as pl
from jax.experimental.pallas import tpu as pltpu
from jax.sharding import PartitionSpec as P

rows_per_block = 16


def shifted(value, axis, steps):
    count = lax.axis_size(axis)
    initial, last = (max(0, -steps), min(count, count - steps))
    return lax.ppermute(value, axis, [(source, source + steps) for source in range(initial, last)])


def partner_swap(value, axis):
    count = lax.axis_size(axis)
    return lax.ppermute(value, axis, [(source, source ^ 1) for source in range(count)])


def chain_kernel(flags, top_ref, incoming_ref, *refs):
    (hidden_u, root_u, b_u, a_u, g_u, hidden_l, root_l, b_l, a_l, g_l,
     source_ref, middle_ref, result_ref, low_u_ref, low_l_ref, pg_u_ref, pg_l_ref) = refs
    rows = incoming_ref.shape[0]
    offset = pl.multiple_of(flags[0] * rows, rows)
    window = pl.ds(offset, rows)
    source = jnp.where(flags[1] == 1, top_ref[window, :], incoming_ref[...])
    source_ref[...] = source

    def one_layer(upstream, hidden_ref, root_ref, b_ref, a_ref, g_ref, low_ref, pg_ref):
        root = root_ref[window, :]
        normalized = hidden_ref[window, :].astype(jnp.float32) / root
        d_low = lax.dot_general(
            upstream, b_ref[...], (((1,), (1,)), ((), ())), preferred_element_type=jnp.float32
        ).astype(jnp.bfloat16)
        normalized_gradient = jnp.dot(d_low, a_ref[...], preferred_element_type=jnp.float32)
        input_gradient = normalized_gradient * g_ref[...]
        mean = jnp.mean(input_gradient * normalized, axis=-1, keepdims=True)
        low_ref[...] = d_low
        pg_ref[...] = jnp.sum(normalized_gradient * normalized, axis=0, keepdims=True)
        return (upstream.astype(jnp.float32) + (input_gradient - normalized * mean) / root).astype(
            jnp.bfloat16
        )

    middle = one_layer(source, hidden_u, root_u, b_u, a_u, g_u, low_u_ref, pg_u_ref)
    middle_ref[...] = middle
    result_ref[...] = one_layer(middle, hidden_l, root_l, b_l, a_l, g_l, low_l_ref, pg_l_ref)


def chain_step(flags, top, incoming, upper, lower, rows):
    width = incoming.shape[1]
    rank = upper[2].shape[0]
    resident = pl.BlockSpec(memory_space=pltpu.VMEM)
    out_shape = [
        jax.ShapeDtypeStruct((rows, width), jnp.bfloat16),
        jax.ShapeDtypeStruct((rows, width), jnp.bfloat16),
        jax.ShapeDtypeStruct((rows, width), jnp.bfloat16),
        jax.ShapeDtypeStruct((rows, rank), jnp.bfloat16),
        jax.ShapeDtypeStruct((rows, rank), jnp.bfloat16),
        jax.ShapeDtypeStruct((1, width), jnp.float32),
        jax.ShapeDtypeStruct((1, width), jnp.float32),
    ]
    return pl.pallas_call(
        chain_kernel,
        out_shape=out_shape,
        in_specs=[pl.BlockSpec(memory_space=pltpu.SMEM)] + [resident] * 12,
        out_specs=[resident] * 7,
        cost_estimate=pl.CostEstimate(
            flops=8 * rows * width * rank, transcendentals=0, bytes_accessed=16 * rows * width
        ),
    )(flags, top, incoming, *upper, *lower)


def on_device(acts, top_grad, a_rows, b_rows, gain):
    sections = lax.axis_size("pipe")
    section = lax.axis_index("pipe")
    pairs = sections // 2
    pair = section // 2
    upper_half = section % 2 == 1
    rank = a_rows.shape[1]
    own_hidden = acts[0, 0]
    rows, width = own_hidden.shape
    half_rows = rows // 2
    my_offset = jnp.where(upper_half, 0, half_rows)
    other_offset = half_rows - my_offset
    own_mine = lax.dynamic_slice_in_dim(own_hidden, my_offset, half_rows, 0)
    partner_rows = partner_swap(lax.dynamic_slice_in_dim(own_hidden, other_offset, half_rows, 0), "pipe")
    hidden_pair = (
        jnp.where(upper_half, own_mine, partner_rows),
        jnp.where(upper_half, partner_rows, own_mine),
    )
    top = lax.dynamic_slice_in_dim(top_grad[0], my_offset, half_rows, 0)
    params = jnp.concatenate([a_rows[0], b_rows[0], gain], axis=0)
    partner_params = partner_swap(params, "pipe")
    stacked = jnp.stack(
        [jnp.where(upper_half, params, partner_params), jnp.where(upper_half, partner_params, params)]
    )
    whole = lax.all_gather(lax.all_gather(stacked, "dp", axis=2, tiled=True), "seq", axis=2, tiled=True)
    contract_last = (((1,), (1,)), ((), ()))
    contract_first = (((0,), (0,)), ((), ()))
    layers = []
    operands = []
    for index in range(2):
        hidden = hidden_pair[index]
        a_full = whole[index, :rank]
        b_full = whole[index, rank : 2 * rank]
        gain_float = whole[index, 2 * rank].astype(jnp.float32)
        hidden_float = hidden.astype(jnp.float32)
        inverse_root_mean = jnp.sqrt(
            jnp.mean(hidden_float * hidden_float, axis=-1, keepdims=True) + 1e-05
        )
        normalized_rows = ((hidden_float / inverse_root_mean) * gain_float).astype(jnp.bfloat16)
        low = jnp.dot(normalized_rows, a_full.T, preferred_element_type=jnp.float32).astype(
            jnp.bfloat16
        )
        layers.append((hidden, inverse_root_mean, low, a_full, b_full, gain_float))
        operands.append((hidden, inverse_root_mean, b_full, a_full, gain_float[None, :]))
    block_total = half_rows // rows_per_block

    def accumulate(layer, source, d_low, part_g, block_offset, sums, inside):
        hidden, inverse_root_mean, low, a_full, b_full, gain_float = layer
        sum_a, sum_b, sum_g = sums
        hidden_part = lax.dynamic_slice_in_dim(hidden, block_offset, rows_per_block, 0)
        r_part = lax.dynamic_slice_in_dim(inverse_root_mean, block_offset, rows_per_block, 0)
        normalized_part = ((hidden_part.astype(jnp.float32) / r_part) * gain_float).astype(jnp.bfloat16)
        low_part = lax.dynamic_slice_in_dim(low, block_offset, rows_per_block, 0)
        part_a = lax.dot_general(
            d_low, normalized_part, contract_first, preferred_element_type=jnp.float32
        )
        part_b = lax.dot_general(low_part, source, contract_first, preferred_element_type=jnp.float32)
        return (
            sum_a + jnp.where(inside, part_a, 0.0),
            sum_b + jnp.where(inside, part_b, 0.0),
            sum_g + jnp.where(inside, part_g, 0.0),
        )

    def turn(turn_index, carry):
        incoming, upper_sums, lower_sums = carry
        block_index = turn_index - (pairs - 1 - pair)
        inside = jnp.logical_and(block_index >= 0, block_index < block_total)
        clipped = jnp.clip(block_index, 0, block_total - 1)
        block_offset = clipped * rows_per_block
        flags = jnp.stack([clipped, (pair == pairs - 1).astype(jnp.int32)]).astype(jnp.int32)
        source, middle, result, low_u, low_l, pg_u, pg_l = chain_step(
            flags, top, incoming, operands[0], operands[1], rows_per_block
        )
        incoming = shifted(result, "pipe", -2)
        upper_sums = accumulate(layers[0], source, low_u, pg_u, block_offset, upper_sums, inside)
        lower_sums = accumulate(layers[1], middle, low_l, pg_l, block_offset, lower_sums, inside)
        return (incoming, upper_sums, lower_sums)

    def zero_sums():
        return (
            jnp.zeros((rank, width), jnp.float32),
            jnp.zeros((rank, width), jnp.float32),
            jnp.zeros((1, width), jnp.float32),
        )

    begin = (jnp.zeros((rows_per_block, width), jnp.bfloat16), zero_sums(), zero_sums())
    _, upper_sums, lower_sums = lax.fori_loop(0, pairs + block_total - 1, turn, begin)
    grads = jnp.stack(
        [jnp.concatenate(upper_sums, axis=0), jnp.concatenate(lower_sums, axis=0)]
    )
    reduced = lax.psum_scatter(grads, "seq", scatter_dimension=2, tiled=True)
    own_layer = jnp.where(upper_half, reduced[0], reduced[1])
    other_layer = jnp.where(upper_half, reduced[1], reduced[0])
    part = own_layer + partner_swap(other_layer, "pipe")
    examples = lax.axis_size("dp")
    example = lax.axis_index("dp")
    square = jnp.sum(part * part)
    total = lax.psum(square, "pipe")
    count = lax.axis_size("seq")
    step = 1
    while step < count:
        total = total + lax.ppermute(
            total, "seq", [(source, (source + step) % count) for source in range(count)]
        )
        step *= 2
    bound = math.sqrt(sections * (2 * rank + 1) * width)
    factor = bound / (jnp.sqrt(total) + 0.01 * bound)
    scaled = factor * part
    share = part.shape[1] // examples
    combined = lax.dynamic_slice_in_dim(scaled, example * share, share, 1)
    for step in range(1, examples):
        target = lax.rem(example + step, examples)
        piece = lax.dynamic_slice_in_dim(scaled, target * share, share, 1)
        combined = combined + lax.ppermute(
            piece, "dp", [(source, (source + step) % examples) for source in range(examples)]
        )
    out_a = combined[:rank]
    out_b = combined[rank : 2 * rank]
    out_g = combined[2 * rank :]
    factor = jnp.reshape(factor, (1,))
    return (out_a[None], out_b[None], out_g, factor)


def solution(mesh):
    in_specs = (
        P("pipe", "dp", "seq", None),
        P("dp", "seq", None),
        P("pipe", None, ("seq", "dp")),
        P("pipe", None, ("seq", "dp")),
        P("pipe", ("seq", "dp")),
    )
    out_specs = (
        P("pipe", None, ("seq", "dp")),
        P("pipe", None, ("seq", "dp")),
        P("pipe", ("seq", "dp")),
        P("dp"),
    )
    return jax.shard_map(
        on_device, mesh=mesh, in_specs=in_specs, out_specs=out_specs, check_vma=False
    )
```

```python
import math

import jax
import jax.numpy as jnp
from jax import lax
from jax.experimental import pallas as pl
from jax.experimental.pallas import tpu as pltpu
from jax.sharding import PartitionSpec as P

rows_per_block = 16


def shifted(value, axis, steps):
    count = lax.axis_size(axis)
    initial, last = (max(0, -steps), min(count, count - steps))
    return lax.ppermute(value, axis, [(source, source + steps) for source in range(initial, last)])


def partner_swap(value, axis):
    count = lax.axis_size(axis)
    return lax.ppermute(value, axis, [(source, source ^ 1) for source in range(count)])


def chain_kernel(flags, top_ref, incoming_ref, *refs):
    (hidden_u, root_u, b_u, a_u, g_u, hidden_l, root_l, b_l, a_l, g_l,
     source_ref, middle_ref, result_ref, low_u_ref, low_l_ref, pg_u_ref, pg_l_ref) = refs
    rows = incoming_ref.shape[0]
    offset = pl.multiple_of(flags[0] * rows, rows)
    window = pl.ds(offset, rows)
    source = jnp.where(flags[1] == 1, top_ref[window, :], incoming_ref[...])
    source_ref[...] = source

    def one_layer(upstream, hidden_ref, root_ref, b_ref, a_ref, g_ref, low_ref, pg_ref):
        root = root_ref[window, :]
        normalized = hidden_ref[window, :].astype(jnp.float32) / root
        d_low = jnp.dot(upstream, b_ref[...], preferred_element_type=jnp.float32).astype(jnp.bfloat16)
        normalized_gradient = jnp.dot(d_low, a_ref[...], preferred_element_type=jnp.float32)
        input_gradient = normalized_gradient * g_ref[...]
        mean = jnp.mean(input_gradient * normalized, axis=-1, keepdims=True)
        low_ref[...] = d_low
        pg_ref[...] = jnp.sum(normalized_gradient * normalized, axis=0, keepdims=True)
        return (upstream.astype(jnp.float32) + (input_gradient - normalized * mean) / root).astype(
            jnp.bfloat16
        )

    middle = one_layer(source, hidden_u, root_u, b_u, a_u, g_u, low_u_ref, pg_u_ref)
    middle_ref[...] = middle
    result_ref[...] = one_layer(middle, hidden_l, root_l, b_l, a_l, g_l, low_l_ref, pg_l_ref)


def chain_step(flags, top, incoming, upper, lower, rows):
    width = incoming.shape[1]
    rank = upper[2].shape[1]
    resident = pl.BlockSpec(memory_space=pltpu.VMEM)
    out_shape = [
        jax.ShapeDtypeStruct((rows, width), jnp.bfloat16),
        jax.ShapeDtypeStruct((rows, width), jnp.bfloat16),
        jax.ShapeDtypeStruct((rows, width), jnp.bfloat16),
        jax.ShapeDtypeStruct((rows, rank), jnp.bfloat16),
        jax.ShapeDtypeStruct((rows, rank), jnp.bfloat16),
        jax.ShapeDtypeStruct((1, width), jnp.float32),
        jax.ShapeDtypeStruct((1, width), jnp.float32),
    ]
    return pl.pallas_call(
        chain_kernel,
        out_shape=out_shape,
        in_specs=[pl.BlockSpec(memory_space=pltpu.SMEM)] + [resident] * 12,
        out_specs=[resident] * 7,
        cost_estimate=pl.CostEstimate(
            flops=8 * rows * width * rank, transcendentals=0, bytes_accessed=16 * rows * width
        ),
    )(flags, top, incoming, *upper, *lower)


def on_device(acts, top_grad, a_rows, b_rows, gain):
    sections = lax.axis_size("pipe")
    section = lax.axis_index("pipe")
    pairs = sections // 2
    pair = section // 2
    upper_half = section % 2 == 1
    rank = a_rows.shape[1]
    own_hidden = acts[0, 0]
    rows, width = own_hidden.shape
    half_rows = rows // 2
    my_offset = jnp.where(upper_half, 0, half_rows)
    other_offset = half_rows - my_offset
    own_mine = lax.dynamic_slice_in_dim(own_hidden, my_offset, half_rows, 0)
    partner_rows = partner_swap(lax.dynamic_slice_in_dim(own_hidden, other_offset, half_rows, 0), "pipe")
    hidden_pair = (
        jnp.where(upper_half, own_mine, partner_rows),
        jnp.where(upper_half, partner_rows, own_mine),
    )
    top = lax.dynamic_slice_in_dim(top_grad[0], my_offset, half_rows, 0)
    params = jnp.concatenate([a_rows[0], b_rows[0], gain], axis=0)
    partner_params = partner_swap(params, "pipe")
    stacked = jnp.stack(
        [jnp.where(upper_half, params, partner_params), jnp.where(upper_half, partner_params, params)]
    )
    whole = lax.all_gather(lax.all_gather(stacked, "dp", axis=2, tiled=True), "seq", axis=2, tiled=True)
    contract_last = (((1,), (1,)), ((), ()))
    contract_first = (((0,), (0,)), ((), ()))
    layers = []
    operands = []
    for index in range(2):
        hidden = hidden_pair[index]
        a_full = whole[index, :rank]
        b_full = whole[index, rank : 2 * rank]
        gain_float = whole[index, 2 * rank].astype(jnp.float32)
        hidden_float = hidden.astype(jnp.float32)
        inverse_root_mean = jnp.sqrt(
            jnp.mean(hidden_float * hidden_float, axis=-1, keepdims=True) + 1e-05
        )
        normalized_rows = ((hidden_float / inverse_root_mean) * gain_float).astype(jnp.bfloat16)
        low = jnp.dot(normalized_rows, a_full.T, preferred_element_type=jnp.float32).astype(
            jnp.bfloat16
        )
        layers.append((hidden, inverse_root_mean, low, a_full, b_full, gain_float))
        operands.append((hidden, inverse_root_mean, b_full.T, a_full, gain_float[None, :]))
    block_total = half_rows // rows_per_block

    def accumulate(layer, source, d_low, part_g, block_offset, sums, inside):
        hidden, inverse_root_mean, low, a_full, b_full, gain_float = layer
        sum_a, sum_b, sum_g = sums
        hidden_part = lax.dynamic_slice_in_dim(hidden, block_offset, rows_per_block, 0)
        r_part = lax.dynamic_slice_in_dim(inverse_root_mean, block_offset, rows_per_block, 0)
        normalized_part = ((hidden_part.astype(jnp.float32) / r_part) * gain_float).astype(jnp.bfloat16)
        low_part = lax.dynamic_slice_in_dim(low, block_offset, rows_per_block, 0)
        part_a = lax.dot_general(
            d_low, normalized_part, contract_first, preferred_element_type=jnp.float32
        )
        part_b = lax.dot_general(low_part, source, contract_first, preferred_element_type=jnp.float32)
        return (
            sum_a + jnp.where(inside, part_a, 0.0),
            sum_b + jnp.where(inside, part_b, 0.0),
            sum_g + jnp.where(inside, part_g, 0.0),
        )

    def turn(turn_index, carry):
        incoming, upper_sums, lower_sums = carry
        block_index = turn_index - (pairs - 1 - pair)
        inside = jnp.logical_and(block_index >= 0, block_index < block_total)
        clipped = jnp.clip(block_index, 0, block_total - 1)
        block_offset = clipped * rows_per_block
        flags = jnp.stack([clipped, (pair == pairs - 1).astype(jnp.int32)]).astype(jnp.int32)
        source, middle, result, low_u, low_l, pg_u, pg_l = chain_step(
            flags, top, incoming, operands[0], operands[1], rows_per_block
        )
        incoming = shifted(result, "pipe", -2)
        upper_sums = accumulate(layers[0], source, low_u, pg_u, block_offset, upper_sums, inside)
        lower_sums = accumulate(layers[1], middle, low_l, pg_l, block_offset, lower_sums, inside)
        return (incoming, upper_sums, lower_sums)

    def zero_sums():
        return (
            jnp.zeros((rank, width), jnp.float32),
            jnp.zeros((rank, width), jnp.float32),
            jnp.zeros((1, width), jnp.float32),
        )

    begin = (jnp.zeros((rows_per_block, width), jnp.bfloat16), zero_sums(), zero_sums())
    _, upper_sums, lower_sums = lax.fori_loop(0, pairs + block_total - 1, turn, begin)
    grads = jnp.stack(
        [jnp.concatenate(upper_sums, axis=0), jnp.concatenate(lower_sums, axis=0)]
    )
    reduced = lax.psum_scatter(grads, "seq", scatter_dimension=2, tiled=True)
    own_layer = jnp.where(upper_half, reduced[0], reduced[1])
    other_layer = jnp.where(upper_half, reduced[1], reduced[0])
    part = own_layer + partner_swap(other_layer, "pipe")
    examples = lax.axis_size("dp")
    example = lax.axis_index("dp")
    square = jnp.sum(part * part)
    total = lax.psum(square, "pipe")
    count = lax.axis_size("seq")
    step = 1
    while step < count:
        total = total + lax.ppermute(
            total, "seq", [(source, (source + step) % count) for source in range(count)]
        )
        step *= 2
    bound = math.sqrt(sections * (2 * rank + 1) * width)
    factor = bound / (jnp.sqrt(total) + 0.01 * bound)
    scaled = factor * part
    share = part.shape[1] // examples
    combined = lax.dynamic_slice_in_dim(scaled, example * share, share, 1)
    for step in range(1, examples):
        target = lax.rem(example + step, examples)
        piece = lax.dynamic_slice_in_dim(scaled, target * share, share, 1)
        combined = combined + lax.ppermute(
            piece, "dp", [(source, (source + step) % examples) for source in range(examples)]
        )
    out_a = combined[:rank]
    out_b = combined[rank : 2 * rank]
    out_g = combined[2 * rank :]
    factor = jnp.reshape(factor, (1,))
    return (out_a[None], out_b[None], out_g, factor)


def solution(mesh):
    in_specs = (
        P("pipe", "dp", "seq", None),
        P("dp", "seq", None),
        P("pipe", None, ("seq", "dp")),
        P("pipe", None, ("seq", "dp")),
        P("pipe", ("seq", "dp")),
    )
    out_specs = (
        P("pipe", None, ("seq", "dp")),
        P("pipe", None, ("seq", "dp")),
        P("pipe", ("seq", "dp")),
        P("dp"),
    )
    return jax.shard_map(
        on_device, mesh=mesh, in_specs=in_specs, out_specs=out_specs, check_vma=False
    )
```

```python
import functools
import math

import jax
import jax.numpy as jnp
from jax import lax
from jax.experimental import pallas as pl
from jax.experimental.pallas import tpu as pltpu
from jax.sharding import PartitionSpec as P

rows_per_block = 16


def shifted(value, axis, steps):
    count = lax.axis_size(axis)
    initial, last = (max(0, -steps), min(count, count - steps))
    return lax.ppermute(value, axis, [(source, source + steps) for source in range(initial, last)])


def partner_swap(value, axis):
    count = lax.axis_size(axis)
    return lax.ppermute(value, axis, [(source, source ^ 1) for source in range(count)])


def chain_kernel(pairs, block_total, turn_ref, top_ref, incoming_ref, *refs):
    (hidden_u, root_u, proj_u, b_u, a_u, g_u, hidden_l, root_l, proj_l, b_l, a_l, g_l,
     source_ref, middle_ref, result_ref, low_u_ref, low_l_ref, pg_u_ref, pg_l_ref) = refs
    rows, width = incoming_ref.shape
    pair = lax.axis_index("pipe") // 2
    block = jnp.clip(turn_ref[0] - (pairs - 1 - pair), 0, block_total - 1)
    window = pl.ds(pl.multiple_of(block * rows, rows), rows)
    source = jnp.where(pair == pairs - 1, top_ref[window, :], incoming_ref[...])
    source_ref[...] = source

    def one_layer(upstream, hidden_ref, root_ref, proj_ref, b_ref, a_ref, g_ref, low_ref, pg_ref):
        root = root_ref[window, :]
        normalized = hidden_ref[window, :].astype(jnp.float32) / root
        d_low = lax.dot_general(
            upstream, b_ref[...], (((1,), (1,)), ((), ())), preferred_element_type=jnp.float32
        ).astype(jnp.bfloat16)
        normalized_gradient = jnp.dot(d_low, a_ref[...], preferred_element_type=jnp.float32)
        input_gradient = normalized_gradient * g_ref[...]
        mean = jnp.sum(d_low.astype(jnp.float32) * proj_ref[window, :], axis=-1, keepdims=True) / width
        low_ref[...] = d_low
        pg_ref[...] = jnp.sum(normalized_gradient * normalized, axis=0, keepdims=True)
        return (upstream.astype(jnp.float32) + (input_gradient - normalized * mean) / root).astype(
            jnp.bfloat16
        )

    middle = one_layer(source, hidden_u, root_u, proj_u, b_u, a_u, g_u, low_u_ref, pg_u_ref)
    middle_ref[...] = middle
    result_ref[...] = one_layer(middle, hidden_l, root_l, proj_l, b_l, a_l, g_l, low_l_ref, pg_l_ref)


def chain_step(turn, top, incoming, upper, lower, pairs, block_total):
    rows, width = incoming.shape
    rank = upper[3].shape[0]
    resident = pl.BlockSpec(memory_space=pltpu.VMEM)
    out_shape = [
        jax.ShapeDtypeStruct((rows, width), jnp.bfloat16),
        jax.ShapeDtypeStruct((rows, width), jnp.bfloat16),
        jax.ShapeDtypeStruct((rows, width), jnp.bfloat16),
        jax.ShapeDtypeStruct((rows, rank), jnp.bfloat16),
        jax.ShapeDtypeStruct((rows, rank), jnp.bfloat16),
        jax.ShapeDtypeStruct((1, width), jnp.float32),
        jax.ShapeDtypeStruct((1, width), jnp.float32),
    ]
    return pl.pallas_call(
        functools.partial(chain_kernel, pairs, block_total),
        out_shape=out_shape,
        in_specs=[pl.BlockSpec(memory_space=pltpu.SMEM)] + [resident] * 14,
        out_specs=[resident] * 7,
        cost_estimate=pl.CostEstimate(
            flops=8 * rows * width * rank, transcendentals=0, bytes_accessed=16 * rows * width
        ),
    )(turn, top, incoming, *upper, *lower)


def on_device(acts, top_grad, a_rows, b_rows, gain):
    sections = lax.axis_size("pipe")
    section = lax.axis_index("pipe")
    pairs = sections // 2
    pair = section // 2
    upper_half = section % 2 == 1
    rank = a_rows.shape[1]
    own_hidden = acts[0, 0]
    rows, width = own_hidden.shape
    half_rows = rows // 2
    my_offset = jnp.where(upper_half, 0, half_rows)
    other_offset = half_rows - my_offset
    own_mine = lax.dynamic_slice_in_dim(own_hidden, my_offset, half_rows, 0)
    partner_rows = partner_swap(lax.dynamic_slice_in_dim(own_hidden, other_offset, half_rows, 0), "pipe")
    hidden_pair = (
        jnp.where(upper_half, own_mine, partner_rows),
        jnp.where(upper_half, partner_rows, own_mine),
    )
    top = lax.dynamic_slice_in_dim(top_grad[0], my_offset, half_rows, 0)
    params = jnp.concatenate([a_rows[0], b_rows[0], gain], axis=0)
    partner_params = partner_swap(params, "pipe")
    stacked = jnp.stack(
        [jnp.where(upper_half, params, partner_params), jnp.where(upper_half, partner_params, params)]
    )
    whole = lax.all_gather(lax.all_gather(stacked, "dp", axis=2, tiled=True), "seq", axis=2, tiled=True)
    contract_last = (((1,), (1,)), ((), ()))
    contract_first = (((0,), (0,)), ((), ()))
    layers = []
    operands = []
    for index in range(2):
        hidden = hidden_pair[index]
        a_full = whole[index, :rank]
        b_full = whole[index, rank : 2 * rank]
        gain_float = whole[index, 2 * rank].astype(jnp.float32)
        hidden_float = hidden.astype(jnp.float32)
        inverse_root_mean = jnp.sqrt(
            jnp.mean(hidden_float * hidden_float, axis=-1, keepdims=True) + 1e-05
        )
        normalized_rows = ((hidden_float / inverse_root_mean) * gain_float).astype(jnp.bfloat16)
        low = jnp.dot(normalized_rows, a_full.T, preferred_element_type=jnp.float32).astype(
            jnp.bfloat16
        )
        layers.append((hidden, inverse_root_mean, low, a_full, b_full, gain_float))
        projection = jnp.dot(
            (hidden_float / inverse_root_mean) * gain_float,
            a_full.astype(jnp.float32).T,
            precision=lax.Precision.HIGHEST,
        )
        operands.append((hidden, inverse_root_mean, projection, b_full, a_full, gain_float[None, :]))
    block_total = half_rows // rows_per_block

    def accumulate(layer, source, d_low, part_g, block_offset, sums, inside):
        hidden, inverse_root_mean, low, a_full, b_full, gain_float = layer
        sum_a, sum_b, sum_g = sums
        hidden_part = lax.dynamic_slice_in_dim(hidden, block_offset, rows_per_block, 0)
        r_part = lax.dynamic_slice_in_dim(inverse_root_mean, block_offset, rows_per_block, 0)
        normalized_part = ((hidden_part.astype(jnp.float32) / r_part) * gain_float).astype(jnp.bfloat16)
        low_part = lax.dynamic_slice_in_dim(low, block_offset, rows_per_block, 0)
        part_a = lax.dot_general(
            d_low, normalized_part, contract_first, preferred_element_type=jnp.float32
        )
        part_b = lax.dot_general(low_part, source, contract_first, preferred_element_type=jnp.float32)
        return (
            sum_a + jnp.where(inside, part_a, 0.0),
            sum_b + jnp.where(inside, part_b, 0.0),
            sum_g + jnp.where(inside, part_g, 0.0),
        )

    def turn(turn_index, carry):
        incoming, upper_sums, lower_sums = carry
        block_index = turn_index - (pairs - 1 - pair)
        inside = jnp.logical_and(block_index >= 0, block_index < block_total)
        clipped = jnp.clip(block_index, 0, block_total - 1)
        block_offset = clipped * rows_per_block
        source, middle, result, low_u, low_l, pg_u, pg_l = chain_step(
            jnp.reshape(turn_index, (1,)).astype(jnp.int32), top, incoming, operands[0], operands[1],
            pairs, block_total,
        )
        incoming = shifted(result, "pipe", -2)
        upper_sums = accumulate(layers[0], source, low_u, pg_u, block_offset, upper_sums, inside)
        lower_sums = accumulate(layers[1], middle, low_l, pg_l, block_offset, lower_sums, inside)
        return (incoming, upper_sums, lower_sums)

    def zero_sums():
        return (
            jnp.zeros((rank, width), jnp.float32),
            jnp.zeros((rank, width), jnp.float32),
            jnp.zeros((1, width), jnp.float32),
        )

    begin = (jnp.zeros((rows_per_block, width), jnp.bfloat16), zero_sums(), zero_sums())
    _, upper_sums, lower_sums = lax.fori_loop(0, pairs + block_total - 1, turn, begin)
    grads = jnp.stack(
        [jnp.concatenate(upper_sums, axis=0), jnp.concatenate(lower_sums, axis=0)]
    )
    reduced = lax.psum_scatter(grads, "seq", scatter_dimension=2, tiled=True)
    own_layer = jnp.where(upper_half, reduced[0], reduced[1])
    other_layer = jnp.where(upper_half, reduced[1], reduced[0])
    part = own_layer + partner_swap(other_layer, "pipe")
    examples = lax.axis_size("dp")
    example = lax.axis_index("dp")
    square = jnp.sum(part * part)
    total = lax.psum(square, "pipe")
    count = lax.axis_size("seq")
    step = 1
    while step < count:
        total = total + lax.ppermute(
            total, "seq", [(source, (source + step) % count) for source in range(count)]
        )
        step *= 2
    bound = math.sqrt(sections * (2 * rank + 1) * width)
    factor = bound / (jnp.sqrt(total) + 0.01 * bound)
    scaled = factor * part
    share = part.shape[1] // examples
    combined = lax.dynamic_slice_in_dim(scaled, example * share, share, 1)
    for step in range(1, examples):
        target = lax.rem(example + step, examples)
        piece = lax.dynamic_slice_in_dim(scaled, target * share, share, 1)
        combined = combined + lax.ppermute(
            piece, "dp", [(source, (source + step) % examples) for source in range(examples)]
        )
    out_a = combined[:rank]
    out_b = combined[rank : 2 * rank]
    out_g = combined[2 * rank :]
    factor = jnp.reshape(factor, (1,))
    return (out_a[None], out_b[None], out_g, factor)


def solution(mesh):
    in_specs = (
        P("pipe", "dp", "seq", None),
        P("dp", "seq", None),
        P("pipe", None, ("seq", "dp")),
        P("pipe", None, ("seq", "dp")),
        P("pipe", ("seq", "dp")),
    )
    out_specs = (
        P("pipe", None, ("seq", "dp")),
        P("pipe", None, ("seq", "dp")),
        P("pipe", ("seq", "dp")),
        P("dp"),
    )
    return jax.shard_map(
        on_device, mesh=mesh, in_specs=in_specs, out_specs=out_specs, check_vma=False
    )
```

```python
import functools
import math

import jax
import jax.numpy as jnp
from jax import lax
from jax.experimental import pallas as pl
from jax.experimental.pallas import tpu as pltpu
from jax.sharding import PartitionSpec as P

rows_per_block = 8


def shifted(value, axis, steps):
    count = lax.axis_size(axis)
    initial, last = (max(0, -steps), min(count, count - steps))
    return lax.ppermute(value, axis, [(source, source + steps) for source in range(initial, last)])


def partner_swap(value, axis):
    count = lax.axis_size(axis)
    return lax.ppermute(value, axis, [(source, source ^ 1) for source in range(count)])


def chain_kernel(pairs, block_total, turn_ref, top_ref, incoming_ref, *refs):
    (hidden_u, root_u, proj_u, b_u, a_u, g_u, hidden_l, root_l, proj_l, b_l, a_l, g_l,
     source_ref, middle_ref, result_ref, low_u_ref, low_l_ref, pg_u_ref, pg_l_ref) = refs
    rows, width = incoming_ref.shape
    pair = lax.axis_index("pipe") // 2
    block = jnp.clip(turn_ref[0] - (pairs - 1 - pair), 0, block_total - 1)
    window = pl.ds(pl.multiple_of(block * rows, rows), rows)
    source = jnp.where(pair == pairs - 1, top_ref[window, :], incoming_ref[...])
    source_ref[...] = source

    def one_layer(upstream, hidden_ref, root_ref, proj_ref, b_ref, a_ref, g_ref, low_ref, pg_ref):
        root = root_ref[window, :]
        normalized = hidden_ref[window, :].astype(jnp.float32) / root
        d_low = lax.dot_general(
            upstream, b_ref[...], (((1,), (1,)), ((), ())), preferred_element_type=jnp.float32
        ).astype(jnp.bfloat16)
        normalized_gradient = jnp.dot(d_low, a_ref[...], preferred_element_type=jnp.float32)
        input_gradient = normalized_gradient * g_ref[...]
        mean = jnp.sum(d_low.astype(jnp.float32) * proj_ref[window, :], axis=-1, keepdims=True) / width
        low_ref[...] = d_low
        pg_ref[...] = jnp.sum(normalized_gradient * normalized, axis=0, keepdims=True)
        return (upstream.astype(jnp.float32) + (input_gradient - normalized * mean) / root).astype(
            jnp.bfloat16
        )

    middle = one_layer(source, hidden_u, root_u, proj_u, b_u, a_u, g_u, low_u_ref, pg_u_ref)
    middle_ref[...] = middle
    result_ref[...] = one_layer(middle, hidden_l, root_l, proj_l, b_l, a_l, g_l, low_l_ref, pg_l_ref)


def chain_step(turn, top, incoming, upper, lower, pairs, block_total):
    rows, width = incoming.shape
    rank = upper[3].shape[0]
    resident = pl.BlockSpec(memory_space=pltpu.VMEM)
    out_shape = [
        jax.ShapeDtypeStruct((rows, width), jnp.bfloat16),
        jax.ShapeDtypeStruct((rows, width), jnp.bfloat16),
        jax.ShapeDtypeStruct((rows, width), jnp.bfloat16),
        jax.ShapeDtypeStruct((rows, rank), jnp.bfloat16),
        jax.ShapeDtypeStruct((rows, rank), jnp.bfloat16),
        jax.ShapeDtypeStruct((1, width), jnp.float32),
        jax.ShapeDtypeStruct((1, width), jnp.float32),
    ]
    return pl.pallas_call(
        functools.partial(chain_kernel, pairs, block_total),
        out_shape=out_shape,
        in_specs=[pl.BlockSpec(memory_space=pltpu.SMEM)] + [resident] * 14,
        out_specs=[resident] * 7,
        cost_estimate=pl.CostEstimate(
            flops=8 * rows * width * rank, transcendentals=0, bytes_accessed=16 * rows * width
        ),
    )(turn, top, incoming, *upper, *lower)


def on_device(acts, top_grad, a_rows, b_rows, gain):
    sections = lax.axis_size("pipe")
    section = lax.axis_index("pipe")
    pairs = sections // 2
    pair = section // 2
    upper_half = section % 2 == 1
    rank = a_rows.shape[1]
    own_hidden = acts[0, 0]
    rows, width = own_hidden.shape
    half_rows = rows // 2
    my_offset = jnp.where(upper_half, 0, half_rows)
    other_offset = half_rows - my_offset
    own_mine = lax.dynamic_slice_in_dim(own_hidden, my_offset, half_rows, 0)
    partner_rows = partner_swap(lax.dynamic_slice_in_dim(own_hidden, other_offset, half_rows, 0), "pipe")
    hidden_pair = (
        jnp.where(upper_half, own_mine, partner_rows),
        jnp.where(upper_half, partner_rows, own_mine),
    )
    top = lax.dynamic_slice_in_dim(top_grad[0], my_offset, half_rows, 0)
    params = jnp.concatenate([a_rows[0], b_rows[0], gain], axis=0)
    partner_params = partner_swap(params, "pipe")
    stacked = jnp.stack(
        [jnp.where(upper_half, params, partner_params), jnp.where(upper_half, partner_params, params)]
    )
    whole = lax.all_gather(lax.all_gather(stacked, "dp", axis=2, tiled=True), "seq", axis=2, tiled=True)
    contract_last = (((1,), (1,)), ((), ()))
    contract_first = (((0,), (0,)), ((), ()))
    layers = []
    operands = []
    for index in range(2):
        hidden = hidden_pair[index]
        a_full = whole[index, :rank]
        b_full = whole[index, rank : 2 * rank]
        gain_float = whole[index, 2 * rank].astype(jnp.float32)
        hidden_float = hidden.astype(jnp.float32)
        inverse_root_mean = jnp.sqrt(
            jnp.mean(hidden_float * hidden_float, axis=-1, keepdims=True) + 1e-05
        )
        normalized_rows = ((hidden_float / inverse_root_mean) * gain_float).astype(jnp.bfloat16)
        low = jnp.dot(normalized_rows, a_full.T, preferred_element_type=jnp.float32).astype(
            jnp.bfloat16
        )
        layers.append((hidden, inverse_root_mean, low, a_full, b_full, gain_float))
        projection = jnp.dot(
            (hidden_float / inverse_root_mean) * gain_float,
            a_full.astype(jnp.float32).T,
            precision=lax.Precision.HIGHEST,
        )
        operands.append((hidden, inverse_root_mean, projection, b_full, a_full, gain_float[None, :]))
    block_total = half_rows // rows_per_block

    def accumulate(layer, source, d_low, part_g, block_offset, sums, inside):
        hidden, inverse_root_mean, low, a_full, b_full, gain_float = layer
        sum_a, sum_b, sum_g = sums
        hidden_part = lax.dynamic_slice_in_dim(hidden, block_offset, rows_per_block, 0)
        r_part = lax.dynamic_slice_in_dim(inverse_root_mean, block_offset, rows_per_block, 0)
        normalized_part = ((hidden_part.astype(jnp.float32) / r_part) * gain_float).astype(jnp.bfloat16)
        low_part = lax.dynamic_slice_in_dim(low, block_offset, rows_per_block, 0)
        part_a = lax.dot_general(
            d_low, normalized_part, contract_first, preferred_element_type=jnp.float32
        )
        part_b = lax.dot_general(low_part, source, contract_first, preferred_element_type=jnp.float32)
        return (
            sum_a + jnp.where(inside, part_a, 0.0),
            sum_b + jnp.where(inside, part_b, 0.0),
            sum_g + jnp.where(inside, part_g, 0.0),
        )

    def turn(turn_index, carry):
        incoming, upper_sums, lower_sums = carry
        block_index = turn_index - (pairs - 1 - pair)
        inside = jnp.logical_and(block_index >= 0, block_index < block_total)
        clipped = jnp.clip(block_index, 0, block_total - 1)
        block_offset = clipped * rows_per_block
        source, middle, result, low_u, low_l, pg_u, pg_l = chain_step(
            jnp.reshape(turn_index, (1,)).astype(jnp.int32), top, incoming, operands[0], operands[1],
            pairs, block_total,
        )
        incoming = shifted(result, "pipe", -2)
        upper_sums = accumulate(layers[0], source, low_u, pg_u, block_offset, upper_sums, inside)
        lower_sums = accumulate(layers[1], middle, low_l, pg_l, block_offset, lower_sums, inside)
        return (incoming, upper_sums, lower_sums)

    def zero_sums():
        return (
            jnp.zeros((rank, width), jnp.float32),
            jnp.zeros((rank, width), jnp.float32),
            jnp.zeros((1, width), jnp.float32),
        )

    begin = (jnp.zeros((rows_per_block, width), jnp.bfloat16), zero_sums(), zero_sums())
    _, upper_sums, lower_sums = lax.fori_loop(0, pairs + block_total - 1, turn, begin)
    grads = jnp.stack(
        [jnp.concatenate(upper_sums, axis=0), jnp.concatenate(lower_sums, axis=0)]
    )
    reduced = lax.psum_scatter(grads, "seq", scatter_dimension=2, tiled=True)
    own_layer = jnp.where(upper_half, reduced[0], reduced[1])
    other_layer = jnp.where(upper_half, reduced[1], reduced[0])
    part = own_layer + partner_swap(other_layer, "pipe")
    examples = lax.axis_size("dp")
    example = lax.axis_index("dp")
    square = jnp.sum(part * part)
    total = lax.psum(square, "pipe")
    count = lax.axis_size("seq")
    step = 1
    while step < count:
        total = total + lax.ppermute(
            total, "seq", [(source, (source + step) % count) for source in range(count)]
        )
        step *= 2
    bound = math.sqrt(sections * (2 * rank + 1) * width)
    factor = bound / (jnp.sqrt(total) + 0.01 * bound)
    scaled = factor * part
    share = part.shape[1] // examples
    combined = lax.dynamic_slice_in_dim(scaled, example * share, share, 1)
    for step in range(1, examples):
        target = lax.rem(example + step, examples)
        piece = lax.dynamic_slice_in_dim(scaled, target * share, share, 1)
        combined = combined + lax.ppermute(
            piece, "dp", [(source, (source + step) % examples) for source in range(examples)]
        )
    out_a = combined[:rank]
    out_b = combined[rank : 2 * rank]
    out_g = combined[2 * rank :]
    factor = jnp.reshape(factor, (1,))
    return (out_a[None], out_b[None], out_g, factor)


def solution(mesh):
    in_specs = (
        P("pipe", "dp", "seq", None),
        P("dp", "seq", None),
        P("pipe", None, ("seq", "dp")),
        P("pipe", None, ("seq", "dp")),
        P("pipe", ("seq", "dp")),
    )
    out_specs = (
        P("pipe", None, ("seq", "dp")),
        P("pipe", None, ("seq", "dp")),
        P("pipe", ("seq", "dp")),
        P("dp"),
    )
    return jax.shard_map(
        on_device, mesh=mesh, in_specs=in_specs, out_specs=out_specs, check_vma=False
    )
```

```python
import functools
import math

import jax
import jax.numpy as jnp
from jax import lax
from jax.experimental import pallas as pl
from jax.experimental.pallas import tpu as pltpu
from jax.sharding import PartitionSpec as P

rows_per_block = 16


def shifted(value, axis, steps):
    count = lax.axis_size(axis)
    initial, last = (max(0, -steps), min(count, count - steps))
    return lax.ppermute(value, axis, [(source, source + steps) for source in range(initial, last)])


def partner_swap(value, axis):
    count = lax.axis_size(axis)
    return lax.ppermute(value, axis, [(source, source ^ 1) for source in range(count)])


def chain_kernel(pairs, block_total, turn_ref, top_ref, incoming_ref, *refs):
    (hidden_u, root_u, proj_u, b_u, a_u, g_u, hidden_l, root_l, proj_l, b_l, a_l, g_l,
     source_ref, middle_ref, result_ref, low_u_ref, low_l_ref, pg_u_ref, pg_l_ref) = refs
    rows, width = incoming_ref.shape
    pair = lax.axis_index("pipe") // 2
    block = jnp.clip(turn_ref[0] - (pairs - 1 - pair), 0, block_total - 1)
    window = pl.ds(pl.multiple_of(block * rows, rows), rows)
    source = jnp.where(pair == pairs - 1, top_ref[window, :], incoming_ref[...])
    source_ref[...] = source

    def one_layer(upstream, hidden_ref, root_ref, proj_ref, b_ref, a_ref, g_ref, low_ref, pg_ref):
        root = root_ref[window, :]
        normalized = hidden_ref[window, :].astype(jnp.float32) / root
        d_low = lax.dot_general(
            upstream, b_ref[...], (((1,), (1,)), ((), ())), preferred_element_type=jnp.float32
        ).astype(jnp.bfloat16)
        normalized_gradient = jnp.dot(d_low, a_ref[...], preferred_element_type=jnp.float32)
        input_gradient = normalized_gradient * g_ref[...]
        mean = jnp.sum(d_low.astype(jnp.float32) * proj_ref[window, :], axis=-1, keepdims=True) / width
        low_ref[...] = d_low
        pg_ref[...] = jnp.sum(normalized_gradient * normalized, axis=0, keepdims=True)
        return (upstream.astype(jnp.float32) + (input_gradient - normalized * mean) / root).astype(
            jnp.bfloat16
        )

    middle = one_layer(source, hidden_u, root_u, proj_u, b_u, a_u, g_u, low_u_ref, pg_u_ref)
    middle_ref[...] = middle
    result_ref[...] = one_layer(middle, hidden_l, root_l, proj_l, b_l, a_l, g_l, low_l_ref, pg_l_ref)


def chain_step(turn, top, incoming, upper, lower, pairs, block_total):
    rows, width = incoming.shape
    rank = upper[3].shape[0]
    resident = pl.BlockSpec(memory_space=pltpu.VMEM)
    out_shape = [
        jax.ShapeDtypeStruct((rows, width), jnp.bfloat16),
        jax.ShapeDtypeStruct((rows, width), jnp.bfloat16),
        jax.ShapeDtypeStruct((rows, width), jnp.bfloat16),
        jax.ShapeDtypeStruct((rows, rank), jnp.bfloat16),
        jax.ShapeDtypeStruct((rows, rank), jnp.bfloat16),
        jax.ShapeDtypeStruct((1, width), jnp.float32),
        jax.ShapeDtypeStruct((1, width), jnp.float32),
    ]
    return pl.pallas_call(
        functools.partial(chain_kernel, pairs, block_total),
        out_shape=out_shape,
        in_specs=[pl.BlockSpec(memory_space=pltpu.SMEM)] + [resident] * 14,
        out_specs=[resident] * 7,
        cost_estimate=pl.CostEstimate(
            flops=8 * rows * width * rank, transcendentals=0, bytes_accessed=16 * rows * width
        ),
    )(turn, top, incoming, *upper, *lower)


def on_device(acts, top_grad, a_rows, b_rows, gain):
    sections = lax.axis_size("pipe")
    section = lax.axis_index("pipe")
    pairs = sections // 2
    pair = section // 2
    upper_half = section % 2 == 1
    rank = a_rows.shape[1]
    own_hidden = acts[0, 0]
    rows, width = own_hidden.shape
    half_rows = rows // 2
    my_offset = jnp.where(upper_half, 0, half_rows)
    other_offset = half_rows - my_offset
    own_mine = lax.dynamic_slice_in_dim(own_hidden, my_offset, half_rows, 0)
    partner_rows = partner_swap(lax.dynamic_slice_in_dim(own_hidden, other_offset, half_rows, 0), "pipe")
    hidden_pair = (
        jnp.where(upper_half, own_mine, partner_rows),
        jnp.where(upper_half, partner_rows, own_mine),
    )
    top = lax.dynamic_slice_in_dim(top_grad[0], my_offset, half_rows, 0)
    params = jnp.concatenate([a_rows[0], b_rows[0], gain], axis=0)
    partner_params = partner_swap(params, "pipe")
    stacked = jnp.stack(
        [jnp.where(upper_half, params, partner_params), jnp.where(upper_half, partner_params, params)]
    )
    whole = lax.all_gather(lax.all_gather(stacked, "dp", axis=2, tiled=True), "seq", axis=2, tiled=True)
    contract_last = (((1,), (1,)), ((), ()))
    contract_first = (((0,), (0,)), ((), ()))
    layers = []
    operands = []
    for index in range(2):
        hidden = hidden_pair[index]
        a_full = whole[index, :rank]
        b_full = whole[index, rank : 2 * rank]
        gain_float = whole[index, 2 * rank].astype(jnp.float32)
        hidden_float = hidden.astype(jnp.float32)
        inverse_root_mean = jnp.sqrt(
            jnp.mean(hidden_float * hidden_float, axis=-1, keepdims=True) + 1e-05
        )
        normalized_rows = ((hidden_float / inverse_root_mean) * gain_float).astype(jnp.bfloat16)
        low = jnp.dot(normalized_rows, a_full.T, preferred_element_type=jnp.float32).astype(
            jnp.bfloat16
        )
        layers.append((hidden, inverse_root_mean, low, a_full, b_full, gain_float))
        projection = jnp.dot(
            (hidden_float / inverse_root_mean) * gain_float,
            a_full.astype(jnp.float32).T,
            precision=lax.Precision.HIGHEST,
        )
        operands.append((hidden, inverse_root_mean, projection, b_full, a_full, gain_float[None, :]))
    block_total = half_rows // rows_per_block

    def accumulate(layer, source, d_low, part_g, block_offset, sums, inside):
        hidden, inverse_root_mean, low, a_full, b_full, gain_float = layer
        sum_a, sum_b, sum_g = sums
        hidden_part = lax.dynamic_slice_in_dim(hidden, block_offset, rows_per_block, 0)
        r_part = lax.dynamic_slice_in_dim(inverse_root_mean, block_offset, rows_per_block, 0)
        normalized_part = ((hidden_part.astype(jnp.float32) / r_part) * gain_float).astype(jnp.bfloat16)
        low_part = lax.dynamic_slice_in_dim(low, block_offset, rows_per_block, 0)
        part_a = lax.dot_general(
            d_low, normalized_part, contract_first, preferred_element_type=jnp.float32
        )
        part_b = lax.dot_general(low_part, source, contract_first, preferred_element_type=jnp.float32)
        return (
            sum_a + jnp.where(inside, part_a, 0.0),
            sum_b + jnp.where(inside, part_b, 0.0),
            sum_g + jnp.where(inside, part_g, 0.0),
        )

    def turn(turn_index, carry):
        incoming, upper_sums, lower_sums = carry
        block_index = turn_index - (pairs - 1 - pair)
        inside = jnp.logical_and(block_index >= 0, block_index < block_total)
        clipped = jnp.clip(block_index, 0, block_total - 1)
        block_offset = clipped * rows_per_block
        source, middle, result, low_u, low_l, pg_u, pg_l = chain_step(
            jnp.reshape(turn_index, (1,)).astype(jnp.int32), top, incoming, operands[0], operands[1],
            pairs, block_total,
        )
        incoming = shifted(result, "pipe", -2)
        upper_sums = accumulate(layers[0], source, low_u, pg_u, block_offset, upper_sums, inside)
        lower_sums = accumulate(layers[1], middle, low_l, pg_l, block_offset, lower_sums, inside)
        return (incoming, upper_sums, lower_sums)

    def zero_sums():
        return (
            jnp.zeros((rank, width), jnp.float32),
            jnp.zeros((rank, width), jnp.float32),
            jnp.zeros((1, width), jnp.float32),
        )

    begin = (jnp.zeros((rows_per_block, width), jnp.bfloat16), zero_sums(), zero_sums())
    _, upper_sums, lower_sums = lax.fori_loop(0, pairs + block_total - 1, turn, begin)
    grads = jnp.stack(
        [jnp.concatenate(upper_sums, axis=0), jnp.concatenate(lower_sums, axis=0)]
    )
    reduced = lax.psum_scatter(grads, "seq", scatter_dimension=2, tiled=True)
    own_layer = jnp.where(upper_half, reduced[0], reduced[1])
    other_layer = jnp.where(upper_half, reduced[1], reduced[0])
    part = own_layer + partner_swap(other_layer, "pipe")
    examples = lax.axis_size("dp")
    example = lax.axis_index("dp")
    share = part.shape[1] // examples
    arrived = []
    for step in range(1, examples):
        target = lax.rem(example + step, examples)
        piece = lax.dynamic_slice_in_dim(part, target * share, share, 1)
        arrived.append(
            lax.ppermute(piece, "dp", [(source, (source + step) % examples) for source in range(examples)])
        )
    square = jnp.sum(part * part)
    total = lax.psum(square, "pipe")
    count = lax.axis_size("seq")
    step = 1
    while step < count:
        total = total + lax.ppermute(
            total, "seq", [(source, (source + step) % count) for source in range(count)]
        )
        step *= 2
    bound = math.sqrt(sections * (2 * rank + 1) * width)
    factor = bound / (jnp.sqrt(total) + 0.01 * bound)
    combined = factor * lax.dynamic_slice_in_dim(part, example * share, share, 1)
    for step, piece in enumerate(arrived, start=1):
        other = lax.ppermute(
            total, "dp", [(source, (source + step) % examples) for source in range(examples)]
        )
        combined = combined + (bound / (jnp.sqrt(other) + 0.01 * bound)) * piece
    out_a = combined[:rank]
    out_b = combined[rank : 2 * rank]
    out_g = combined[2 * rank :]
    factor = jnp.reshape(factor, (1,))
    return (out_a[None], out_b[None], out_g, factor)


def solution(mesh):
    in_specs = (
        P("pipe", "dp", "seq", None),
        P("dp", "seq", None),
        P("pipe", None, ("seq", "dp")),
        P("pipe", None, ("seq", "dp")),
        P("pipe", ("seq", "dp")),
    )
    out_specs = (
        P("pipe", None, ("seq", "dp")),
        P("pipe", None, ("seq", "dp")),
        P("pipe", ("seq", "dp")),
        P("dp"),
    )
    return jax.shard_map(
        on_device, mesh=mesh, in_specs=in_specs, out_specs=out_specs, check_vma=False
    )
```
